256 devices in a mesh: row: 32 (over y, x, z_hi), col: 8 (over z_lo, core).
Axes of the slice: x: 4, y: 4, z: 8 (z_hi: 2, z_lo: 4; z = z_hi * 4 + z_lo), core: 2. Of those that a mesh axis runs over, the one named last changes fastest.
Arguments:
- rhs: float32 [32, 8, 12, 192, 128], P('row', 'col'), may hold values from -6 to 6
- smoother: bfloat16 [32, 8, 3, 3, 768], P('row', 'col'), may hold values from -0.375 to 2.375
- blocks: bfloat16 [32, 8, 12, 192, 1536], P('row', 'col'), may hold values from -0.15625 to 0.15625
- col_index: int32 [32, 8, 12, 8], P('row', 'col'), may hold values from 0 to 27, as said below
- send_list: int32 [32, 8, 4, 4], P('row', 'col'), may hold values from 0 to 11, as said below
- agg_id: int32 [32, 8, 12], P('row', 'col'), may hold values from 0 to 3, as said below
- prolong: bfloat16 [32, 8, 6, 2304], P('row', 'col'), may hold values from -0.4375 to 0.4375
- coarse_inverse: bfloat16 [6144, 6144], P('row'), may hold values from -0.078125 to 0.078125
Outputs:
- smoothed_solution: float32 [32, 8, 12, 192, 128], P('row', 'col')
The draws below stay inside these ranges and needn't reach their ends.
Inputs may be any that keep to these rules, and one draw needn't show every extreme that they name: `col_index`: A value below 12 names a block row of the same device; the value 12 + 4 * g + j names slot j of ghost group g. Every ghost slot is named by some entry of each device. `send_list`: the 4 blocks of one device and group are distinct. `agg_id`: every aggregate of a device holds at least one block row.
All inputs are finite; a program needn't handle non-finite values.
Results may differ from the reference program's by a relative error of at most 0.0029.
Values may be sent and summed in bfloat16 or wider, within the bound.
No kernel may reach another device: no remote copies, remote signals or barrier semaphores. Data moves between devices by JAX's collectives and lax.ppermute only.
A program may use at most 64 MiB of HBM per device.

```python
import math
import jax
import jax.numpy as jnp
from jax import lax

GR = 64
DOF = 192
K = 8
NB = 12
NRHS = 128
CD = 6
HB = 4
AGG_DEV = 4
NC = 6144
N_ROW = 32
N_COL = 8


def distinct_ranks(key, leading, entries):
    scores = jax.random.randint(key, leading + (entries,), 0, 1 << 20, dtype=jnp.int32) * entries
    scores = scores + jnp.arange(entries, dtype=jnp.int32)
    ordering = jnp.argsort(scores, axis=-1).astype(jnp.int32)
    position = jnp.argsort(ordering, axis=-1).astype(jnp.int32)
    return (position, ordering)


def draw_smoother(key, part):
    key_spread = jax.random.fold_in(key, 1)
    key_diagonal = jax.random.fold_in(key, 2)
    full_shape = (N_ROW, N_COL, 3, 3, NB * GR)
    spread = jax.random.uniform(key_spread, full_shape, jnp.float32, -0.375, 0.375)
    diagonal = jnp.exp(jax.random.uniform(key_diagonal, full_shape, jnp.float32, math.log(0.5), math.log(2.0)))
    identity = (jnp.arange(3)[:, None] == jnp.arange(3)[None, :]).astype(jnp.float32)[None, None, :, :, None]
    return (spread + identity * diagonal).astype(jnp.bfloat16)


def draw_col_index(key, part):
    entries = NB * K
    ghost_slots = 4 * HB
    position, ordering = distinct_ranks(jax.random.fold_in(key, 11), (N_ROW, N_COL), entries)
    filler = jax.random.randint(jax.random.fold_in(key, 12), (N_ROW, N_COL, entries), 0, NB + ghost_slots, dtype=jnp.int32)
    values = jnp.where(position < ghost_slots, NB + position, filler)
    return values.reshape((N_ROW, N_COL, NB, K)).astype(jnp.int32)


def draw_send_list(key, part):
    position, ordering = distinct_ranks(jax.random.fold_in(key, 21), (N_ROW, N_COL, 4), NB)
    return ordering[:, :, :, :HB].astype(jnp.int32)


def draw_agg_id(key, part):
    position, ordering = distinct_ranks(jax.random.fold_in(key, 31), (N_ROW, N_COL), NB)
    filler = jax.random.randint(jax.random.fold_in(key, 32), (N_ROW, N_COL, NB), 0, AGG_DEV, dtype=jnp.int32)
    return jnp.where(position < AGG_DEV, position, filler).astype(jnp.int32)


def block_scale(stream_key, shape, shards, low, high):
    def one(axis_at, shards_of):
        steps = jax.random.uniform(jax.random.fold_in(jax.random.fold_in(stream_key, 6), axis_at), (shards_of,), jnp.float32, low / len(shards), high / len(shards))
        return jnp.repeat(jnp.exp(steps), shape[axis_at] // shards_of).reshape((-1,) + (1,) * (len(shape) - axis_at - 1))

    loudness = one(*shards[0])
    for cut in shards[1:]:
        loudness = loudness * one(*cut)
    return loudness


def bell_draw(key, shape, scale, limit, cuts=(), kind=jnp.bfloat16):
    gain = block_scale(key, shape, cuts, -0.22, 0.18) if cuts else 1.0
    drawn = jax.random.normal(key, shape, jnp.float32) * scale * gain
    return jnp.minimum(jnp.maximum(drawn, -limit), limit).astype(kind)


def setup_inputs(seed: int = 0) -> dict:
    keys = jax.random.split(jax.random.key(seed), 9)
    return {
        "rhs": bell_draw(keys[0], (N_ROW, N_COL, NB, DOF, NRHS), 1.0, 6.0, ((0, 32), (1, 8)), jnp.float32),
        "smoother": draw_smoother(jax.random.fold_in(keys[8], 71), 0),
        "blocks": bell_draw(keys[2], (N_ROW, N_COL, NB, DOF, K * DOF), (K * DOF) ** -0.5, 0.15625, ((0, 32), (1, 8))),
        "col_index": draw_col_index(jax.random.fold_in(keys[8], 71), 0),
        "send_list": draw_send_list(jax.random.fold_in(keys[8], 71), 0),
        "agg_id": draw_agg_id(jax.random.fold_in(keys[8], 71), 0),
        "prolong": bell_draw(keys[6], (N_ROW, N_COL, CD, NB * DOF), DOF ** -0.5, 0.4375, ((0, 32), (1, 8))),
        "coarse_inverse": bell_draw(keys[7], (NC, NC), NC ** -0.5, 0.078125, ((0, 32),)),
    }


damping = 0.6


def point_smooth(coefficients, vector):
    leading = vector.shape[:2]
    blocks = vector.shape[2]
    grains = vector.shape[3] // 3
    columns = vector.shape[4]
    factors = coefficients.astype(jnp.float32).reshape(leading + (3, 3, blocks, grains))
    pieces = vector.reshape(leading + (blocks, 3, grains, columns))
    outputs = []
    for component in range(3):
        summed = factors[:, :, component, 0, :, :, None] * pieces[:, :, :, 0]
        summed = summed + factors[:, :, component, 1, :, :, None] * pieces[:, :, :, 1]
        summed = summed + factors[:, :, component, 2, :, :, None] * pieces[:, :, :, 2]
        outputs.append(summed)
    return damping * jnp.stack(outputs, axis=3).reshape(vector.shape)


def ghost_sources(vector_low, send_list):
    stacked = [vector_low]
    moves = ((1, 0), (-1, 0), (1, 1), (-1, 1))
    for group in range(4):
        amount, along = moves[group]
        rolled_vector = jnp.roll(vector_low, amount, axis=along)
        rolled_list = jnp.roll(send_list[:, :, group], amount, axis=along)
        stacked.append(jnp.take_along_axis(rolled_vector, rolled_list[:, :, :, None, None], axis=2))
    return jnp.concatenate(stacked, axis=2)


def apply_operator(blocks, col_index, send_list, vector):
    vector_low = vector.astype(jnp.bfloat16)
    source = ghost_sources(vector_low, send_list)
    device_count = N_ROW * N_COL
    flat_blocks = blocks.reshape((device_count,) + blocks.shape[2:])
    flat_index = col_index.reshape((device_count,) + col_index.shape[2:])
    flat_source = source.reshape((device_count,) + source.shape[2:])

    def device_product(operands):
        matrix, columns, gathered = operands
        picked = jnp.take(gathered, columns.reshape(-1), axis=0)
        picked = picked.reshape((columns.shape[0], -1, gathered.shape[-1]))
        return jnp.einsum("nde,ner->ndr", matrix.astype(jnp.float32), picked.astype(jnp.float32),
                          precision=lax.Precision.HIGHEST)

    result = lax.map(device_product, (flat_blocks, flat_index, flat_source))
    return result.reshape(vector.shape)


def reference(rhs, smoother, blocks, col_index, send_list, agg_id, prolong, coarse_inverse):
    first_iter = point_smooth(smoother, rhs)
    residual_first = rhs - apply_operator(blocks, col_index, send_list, first_iter)
    update_second = point_smooth(smoother, residual_first)
    second_iter = first_iter + update_second
    residual_second = residual_first - apply_operator(blocks, col_index, send_list, update_second)
    shaped = prolong.astype(jnp.float32).reshape((N_ROW, N_COL, CD, NB, DOF))
    residual_low = lax.optimization_barrier(residual_second.astype(jnp.bfloat16))
    local_terms = jnp.einsum("abknd,abndr->abnkr", shaped, residual_low.astype(jnp.float32),
                             precision=lax.Precision.HIGHEST)
    onehot = (agg_id[:, :, None, :] == jnp.arange(AGG_DEV, dtype=jnp.int32)[None, None, :, None]).astype(jnp.float32)
    coarse_residual = jnp.einsum("abxn,abnkr->abxkr", onehot, local_terms, precision=lax.Precision.HIGHEST)
    coarse_rhs = coarse_residual.astype(jnp.bfloat16).reshape((NC, NRHS))
    coarse_solution = jnp.dot(coarse_inverse, coarse_rhs, preferred_element_type=jnp.float32)
    coarse_rounded = coarse_solution.astype(jnp.bfloat16).reshape((N_ROW, N_COL, AGG_DEV, CD, NRHS))
    coarse_rounded = lax.optimization_barrier(coarse_rounded)
    picked = jnp.take_along_axis(coarse_rounded, agg_id[:, :, :, None, None], axis=2)
    correction = jnp.einsum("abknd,abnkr->abndr", shaped, picked.astype(jnp.float32),
                            precision=lax.Precision.HIGHEST)
    after_coarse = second_iter + correction
    residual_third = residual_second - apply_operator(blocks, col_index, send_list, correction)
    return after_coarse + point_smooth(smoother, residual_third)
```

```python
import functools

import jax
import jax.numpy as jnp
from jax import lax
from jax.experimental import pallas as pl
from jax.experimental.pallas import tpu as pltpu
from jax.sharding import PartitionSpec as P

damping = 0.6


def passed_along(value, axis, steps):
    count = lax.axis_size(axis)
    pairs = [(source, (source + steps) % count) for source in range(count)]
    return lax.ppermute(value, axis, pairs)


def point_smooth(coefficients, vector):
    leading = vector.shape[:2]
    blocks = vector.shape[2]
    grains = vector.shape[3] // 3
    columns = vector.shape[4]
    factors = coefficients.astype(jnp.float32).reshape(leading + (3, 3, blocks, grains))
    pieces = vector.reshape(leading + (blocks, 3, grains, columns))
    outputs = []
    for component in range(3):
        summed = factors[:, :, component, 0, :, :, None] * pieces[:, :, :, 0]
        summed = summed + factors[:, :, component, 1, :, :, None] * pieces[:, :, :, 1]
        summed = summed + factors[:, :, component, 2, :, :, None] * pieces[:, :, :, 2]
        outputs.append(summed)
    return damping * jnp.stack(outputs, axis=3).reshape(vector.shape)


def product_kernel(stored, columns_ref, blocks_ref, source_ref, out_ref, picked):
    n = pl.program_id(0)
    dof = source_ref.shape[1]
    for k in range(stored):
        picked[k * dof:(k + 1) * dof, :] = source_ref[columns_ref[n * stored + k]]
    out_ref[0] = jnp.dot(blocks_ref[0], picked[...], preferred_element_type=jnp.float32)


def block_product(blocks, columns, source):
    block_count, dof, width = blocks.shape
    stored = width // dof
    vectors = source.shape[-1]
    grid_spec = pltpu.PrefetchScalarGridSpec(
        num_scalar_prefetch=1,
        grid=(block_count,),
        in_specs=[
            pl.BlockSpec((1, dof, width), lambda n, c: (n, 0, 0)),
            pl.BlockSpec(source.shape, lambda n, c: (0, 0, 0)),
        ],
        out_specs=pl.BlockSpec((1, dof, vectors), lambda n, c: (n, 0, 0)),
        scratch_shapes=[pltpu.VMEM((width, vectors), source.dtype)],
    )
    flops = 2 * block_count * dof * width * vectors
    moved = blocks.size * 2 + source.size * 2 + block_count * dof * vectors * 4
    return pl.pallas_call(
        functools.partial(product_kernel, stored),
        grid_spec=grid_spec,
        out_shape=jax.ShapeDtypeStruct((block_count, dof, vectors), jnp.float32),
        cost_estimate=pl.CostEstimate(flops=flops, bytes_accessed=moved, transcendentals=0),
    )(columns.reshape(-1), blocks, source)


def gathered_copies(value, axis):
    count = lax.axis_size(axis)
    repeated = jnp.broadcast_to(value[None], (count,) + value.shape)
    repeated = repeated.reshape((count * value.shape[0],) + value.shape[1:])
    return lax.all_to_all(repeated, axis, 0, 0, tiled=True)


def body(rhs, smoother, blocks, col_index, send_list, agg_id, prolong, coarse_inverse):
    block_count = rhs.shape[2]
    dof_count = rhs.shape[3]
    vectors = rhs.shape[4]
    send_rows = send_list[0, 0]
    coarse_dofs = prolong.shape[2]
    shaped = prolong[0, 0].reshape((coarse_dofs, block_count, dof_count))
    local_blocks = blocks[0, 0]
    columns = col_index[0, 0]

    def apply_operator(vector):
        vector_low = vector.astype(jnp.bfloat16)
        shard_low = vector_low[0, 0]
        ghosts = []
        for offset in (1, -1):
            packed = jnp.take(shard_low, send_rows[0 if offset == 1 else 1], axis=0)
            ghosts.append(passed_along(packed, "row", offset))
        for offset in (1, -1):
            packed = jnp.take(shard_low, send_rows[2 if offset == 1 else 3], axis=0)
            ghosts.append(passed_along(packed, "col", offset))
        source = jnp.concatenate([shard_low] + list(ghosts), axis=0)
        return block_product(local_blocks, columns, source)[None, None]

    first_iter = point_smooth(smoother, rhs)
    residual_first = rhs - apply_operator(first_iter)
    update_second = point_smooth(smoother, residual_first)
    second_iter = first_iter + update_second
    residual_second = residual_first - apply_operator(update_second)
    row_count = lax.axis_size("row")
    col_count = lax.axis_size("col")
    coarse_rows = coarse_inverse.shape[1] // (row_count * col_count)
    aggregates = coarse_rows // coarse_dofs
    onehot = (agg_id[0, 0][None, :] == jnp.arange(aggregates, dtype=jnp.int32)[:, None]).astype(
        jnp.float32
    )
    local_terms = jnp.einsum(
        "knd,ndr->nkr",
        shaped,
        residual_second[0, 0].astype(jnp.bfloat16),
        preferred_element_type=jnp.float32,
    )
    coarse_residual = jnp.einsum(
        "an,nkr->akr", onehot, local_terms, precision=lax.Precision.HIGHEST
    )
    coarse_rhs = coarse_residual.astype(jnp.bfloat16).reshape((coarse_rows, vectors))
    column_part = gathered_copies(coarse_rhs, "row")
    held = coarse_inverse.reshape((coarse_inverse.shape[0], row_count, col_count, coarse_rows))
    held = lax.dynamic_slice_in_dim(held, lax.axis_index("col"), 1, 2)
    held = held.reshape((coarse_inverse.shape[0], row_count * coarse_rows))
    partial = jnp.dot(held, column_part, preferred_element_type=jnp.float32)
    partial = lax.all_to_all(partial, "col", 0, 0, tiled=True)
    coarse_solution = partial.reshape((col_count, coarse_rows, vectors)).sum(axis=0)
    coarse_rounded = coarse_solution.astype(jnp.bfloat16).reshape(
        (aggregates, coarse_dofs, vectors)
    )
    chosen = jnp.einsum(
        "an,akr->nkr",
        onehot.astype(jnp.bfloat16),
        coarse_rounded,
        preferred_element_type=jnp.float32,
    ).astype(jnp.bfloat16)
    correction = jnp.einsum("knd,nkr->ndr", shaped, chosen, preferred_element_type=jnp.float32)[
        None, None
    ]
    after_coarse = second_iter + correction
    residual_third = residual_second - apply_operator(correction)
    return after_coarse + point_smooth(smoother, residual_third)


def solution(mesh):
    placed = (
        P("row", "col", None, None, None),
        P("row", "col", None, None, None),
        P("row", "col", None, None, None),
        P("row", "col", None, None),
        P("row", "col", None, None),
        P("row", "col", None),
        P("row", "col", None, None),
        P("row", None),
    )
    return jax.shard_map(
        body,
        mesh=mesh,
        in_specs=placed,
        out_specs=P("row", "col", None, None, None),
        check_vma=False,
    )
```

```python
import functools

import jax
import jax.numpy as jnp
from jax import lax
from jax.experimental import pallas as pl
from jax.experimental.pallas import tpu as pltpu
from jax.sharding import PartitionSpec as P

damping = 0.6


def passed_along(value, axis, steps):
    count = lax.axis_size(axis)
    pairs = [(source, (source + steps) % count) for source in range(count)]
    return lax.ppermute(value, axis, pairs)


def point_smooth(coefficients, vector):
    leading = vector.shape[:2]
    blocks = vector.shape[2]
    grains = vector.shape[3] // 3
    columns = vector.shape[4]
    factors = coefficients.astype(jnp.float32).reshape(leading + (3, 3, blocks, grains))
    pieces = vector.reshape(leading + (blocks, 3, grains, columns))
    outputs = []
    for component in range(3):
        summed = factors[:, :, component, 0, :, :, None] * pieces[:, :, :, 0]
        summed = summed + factors[:, :, component, 1, :, :, None] * pieces[:, :, :, 1]
        summed = summed + factors[:, :, component, 2, :, :, None] * pieces[:, :, :, 2]
        outputs.append(summed)
    return damping * jnp.stack(outputs, axis=3).reshape(vector.shape)


def product_kernel(stored, rows, columns_ref, blocks_ref, source_ref, out_ref, picked):
    n = pl.program_id(0)
    dof = source_ref.shape[1]
    for j in range(rows):
        for k in range(stored):
            picked[k * dof:(k + 1) * dof, :] = source_ref[columns_ref[(n * rows + j) * stored + k]]
        out_ref[j] = jnp.dot(blocks_ref[j], picked[...], preferred_element_type=jnp.float32)


def block_product(blocks, columns, source):
    block_count, dof, width = blocks.shape
    stored = width // dof
    vectors = source.shape[-1]
    rows = 6 if block_count % 6 == 0 else 1
    grid_spec = pltpu.PrefetchScalarGridSpec(
        num_scalar_prefetch=1,
        grid=(block_count // rows,),
        in_specs=[
            pl.BlockSpec((rows, dof, width), lambda n, c: (n, 0, 0)),
            pl.BlockSpec(source.shape, lambda n, c: (0, 0, 0)),
        ],
        out_specs=pl.BlockSpec((rows, dof, vectors), lambda n, c: (n, 0, 0)),
        scratch_shapes=[pltpu.VMEM((width, vectors), source.dtype)],
    )
    flops = 2 * block_count * dof * width * vectors
    moved = blocks.size * 2 + source.size * 2 + block_count * dof * vectors * 4
    return pl.pallas_call(
        functools.partial(product_kernel, stored, rows),
        grid_spec=grid_spec,
        out_shape=jax.ShapeDtypeStruct((block_count, dof, vectors), jnp.float32),
        cost_estimate=pl.CostEstimate(flops=flops, bytes_accessed=moved, transcendentals=0),
    )(columns.reshape(-1), blocks, source)


def gathered_copies(value, axis):
    count = lax.axis_size(axis)
    repeated = jnp.broadcast_to(value[None], (count,) + value.shape)
    repeated = repeated.reshape((count * value.shape[0],) + value.shape[1:])
    return lax.all_to_all(repeated, axis, 0, 0, tiled=True)


def exchange(parts):
    return [
        passed_along(parts[0], "row", 1),
        passed_along(parts[1], "row", -1),
        passed_along(parts[2], "col", 1),
        passed_along(parts[3], "col", -1),
    ]


def body(rhs, smoother, blocks, col_index, send_list, agg_id, prolong, coarse_inverse):
    block_count = rhs.shape[2]
    dof_count = rhs.shape[3]
    vectors = rhs.shape[4]
    send_rows = send_list[0, 0]
    groups, ghost_count = send_rows.shape
    coarse_dofs = prolong.shape[2]
    shaped = prolong[0, 0].reshape((coarse_dofs, block_count, dof_count))
    local_blocks = blocks[0, 0]
    columns = col_index[0, 0]
    row_count = lax.axis_size("row")
    col_count = lax.axis_size("col")
    coarse_rows = coarse_inverse.shape[1] // (row_count * col_count)
    aggregates = coarse_rows // coarse_dofs
    onehot = (agg_id[0, 0][None, :] == jnp.arange(aggregates, dtype=jnp.int32)[:, None]).astype(
        jnp.float32
    )

    def outgoing(vector):
        shard_low = vector.astype(jnp.bfloat16)[0, 0]
        packed = jnp.take(shard_low, send_rows.reshape(-1), axis=0)
        parts = [packed[g * ghost_count:(g + 1) * ghost_count] for g in range(groups)]
        return shard_low, parts

    def product(shard_low, ghosts):
        source = jnp.concatenate([shard_low] + list(ghosts), axis=0)
        return block_product(local_blocks, columns, source)[None, None]

    tables = []
    for g in range(groups):
        picked = jnp.take(shaped, send_rows[g], axis=1)
        member = jnp.take(onehot, send_rows[g], axis=1).astype(jnp.bfloat16)
        table = member.T[:, :, None, None] * jnp.transpose(picked, (1, 0, 2))[:, None, :, :]
        tables.append(table.reshape((ghost_count * coarse_rows * dof_count) // vectors, vectors))
    ghost_rows = ghost_count * dof_count

    first_iter = point_smooth(smoother, rhs)
    shard_low, parts = outgoing(first_iter)
    payloads = [
        jnp.concatenate([parts[g].reshape(ghost_rows, vectors), tables[g]], axis=0)
        for g in range(groups)
    ]
    arrived = exchange(payloads)
    ghosts = [a[:ghost_rows].reshape((ghost_count, dof_count, vectors)) for a in arrived]
    neighbour_tables = [
        a[ghost_rows:].reshape((ghost_count, coarse_rows, dof_count)) for a in arrived
    ]
    residual_first = rhs - product(shard_low, ghosts)
    update_second = point_smooth(smoother, residual_first)
    second_iter = first_iter + update_second
    shard_low, parts = outgoing(update_second)
    residual_second = residual_first - product(shard_low, exchange(parts))
    local_terms = jnp.einsum(
        "knd,ndr->nkr",
        shaped,
        residual_second[0, 0].astype(jnp.bfloat16),
        preferred_element_type=jnp.float32,
    )
    coarse_residual = jnp.einsum(
        "an,nkr->akr", onehot, local_terms, precision=lax.Precision.HIGHEST
    )
    coarse_rhs = coarse_residual.astype(jnp.bfloat16).reshape((coarse_rows, vectors))
    column_part = gathered_copies(coarse_rhs, "row")
    held = coarse_inverse.reshape((coarse_inverse.shape[0], row_count, col_count, coarse_rows))
    held = lax.dynamic_slice_in_dim(held, lax.axis_index("col"), 1, 2)
    held = held.reshape((coarse_inverse.shape[0], row_count * coarse_rows))
    partial = jnp.dot(held, column_part, preferred_element_type=jnp.float32)
    partial = lax.all_to_all(partial, "col", 0, 0, tiled=True)
    coarse_solution = partial.reshape((col_count, coarse_rows, vectors)).sum(axis=0)
    coarse_flat = coarse_solution.astype(jnp.bfloat16)
    coarse_rounded = coarse_flat.reshape((aggregates, coarse_dofs, vectors))
    neighbour_coarse = exchange([coarse_flat] * groups)
    chosen = jnp.einsum(
        "an,akr->nkr",
        onehot.astype(jnp.bfloat16),
        coarse_rounded,
        preferred_element_type=jnp.float32,
    ).astype(jnp.bfloat16)
    correction = jnp.einsum("knd,nkr->ndr", shaped, chosen, preferred_element_type=jnp.float32)[
        None, None
    ]
    after_coarse = second_iter + correction
    ghost_corrections = [
        jnp.einsum(
            "bjd,jr->bdr", neighbour_tables[g], neighbour_coarse[g],
            preferred_element_type=jnp.float32,
        ).astype(jnp.bfloat16)
        for g in range(groups)
    ]
    correction_low = correction.astype(jnp.bfloat16)[0, 0]
    residual_third = residual_second - product(correction_low, ghost_corrections)
    return after_coarse + point_smooth(smoother, residual_third)


def solution(mesh):
    placed = (
        P("row", "col", None, None, None),
        P("row", "col", None, None, None),
        P("row", "col", None, None, None),
        P("row", "col", None, None),
        P("row", "col", None, None),
        P("row", "col", None),
        P("row", "col", None, None),
        P("row", None),
    )
    return jax.shard_map(
        body,
        mesh=mesh,
        in_specs=placed,
        out_specs=P("row", "col", None, None, None),
        check_vma=False,
    )
```

```python
import functools

import jax
import jax.numpy as jnp
from jax import lax
from jax.experimental import pallas as pl
from jax.experimental.pallas import tpu as pltpu
from jax.sharding import PartitionSpec as P

damping = 0.6


def passed_along(value, axis, steps):
    count = lax.axis_size(axis)
    pairs = [(source, (source + steps) % count) for source in range(count)]
    return lax.ppermute(value, axis, pairs)


def point_smooth(coefficients, vector):
    leading = vector.shape[:2]
    blocks = vector.shape[2]
    grains = vector.shape[3] // 3
    columns = vector.shape[4]
    factors = coefficients.astype(jnp.float32).reshape(leading + (3, 3, blocks, grains))
    pieces = vector.reshape(leading + (blocks, 3, grains, columns))
    outputs = []
    for component in range(3):
        summed = factors[:, :, component, 0, :, :, None] * pieces[:, :, :, 0]
        summed = summed + factors[:, :, component, 1, :, :, None] * pieces[:, :, :, 1]
        summed = summed + factors[:, :, component, 2, :, :, None] * pieces[:, :, :, 2]
        outputs.append(summed)
    return damping * jnp.stack(outputs, axis=3).reshape(vector.shape)


def product_kernel(stored, rows, columns_ref, blocks_ref, prev_ref, local_ref, *rest):
    ghost_refs = rest[:-3]
    out_ref, source, picked = rest[-3:]
    n = pl.program_id(0)
    block_count, dof = local_ref.shape[0], local_ref.shape[1]
    ghost_count = (source.shape[0] - block_count) // len(ghost_refs)

    @pl.when(n == 0)
    def _():
        source[0:block_count] = local_ref[...]
        for g, ref in enumerate(ghost_refs):
            for b in range(ghost_count):
                source[block_count + g * ghost_count + b] = ref[b * dof:(b + 1) * dof, :]

    for j in range(rows):
        for k in range(stored):
            picked[k * dof:(k + 1) * dof, :] = source[columns_ref[(n * rows + j) * stored + k]]
        out_ref[j] = prev_ref[j] - jnp.dot(
            blocks_ref[j], picked[...], preferred_element_type=jnp.float32
        )


def block_product(blocks, columns, prev, local, ghosts, ghost_count):
    block_count, dof, width = blocks.shape
    stored = width // dof
    vectors = local.shape[-1]
    rows = 6 if block_count % 6 == 0 else 1
    whole = lambda shape: pl.BlockSpec(shape, lambda n, c: (0,) * len(shape))
    grid_spec = pltpu.PrefetchScalarGridSpec(
        num_scalar_prefetch=1,
        grid=(block_count // rows,),
        in_specs=[
            pl.BlockSpec((rows, dof, width), lambda n, c: (n, 0, 0)),
            pl.BlockSpec((rows, dof, vectors), lambda n, c: (n, 0, 0)),
            whole(local.shape),
        ]
        + [whole(g.shape) for g in ghosts],
        out_specs=pl.BlockSpec((rows, dof, vectors), lambda n, c: (n, 0, 0)),
        scratch_shapes=[
            pltpu.VMEM((block_count + len(ghosts) * ghost_count, dof, vectors), local.dtype),
            pltpu.VMEM((width, vectors), local.dtype),
        ],
    )
    flops = 2 * block_count * dof * width * vectors
    moved = blocks.size * 2 + local.size * 2 * 3 + prev.size * 8
    return pl.pallas_call(
        functools.partial(product_kernel, stored, rows),
        grid_spec=grid_spec,
        out_shape=jax.ShapeDtypeStruct((block_count, dof, vectors), jnp.float32),
        cost_estimate=pl.CostEstimate(flops=flops, bytes_accessed=moved, transcendentals=0),
    )(columns.reshape(-1), blocks, prev, local, *ghosts)


def gathered_copies(value, axis):
    count = lax.axis_size(axis)
    repeated = jnp.broadcast_to(value[None], (count,) + value.shape)
    repeated = repeated.reshape((count * value.shape[0],) + value.shape[1:])
    return lax.all_to_all(repeated, axis, 0, 0, tiled=True)


def exchange(parts):
    return [
        passed_along(parts[0], "row", 1),
        passed_along(parts[1], "row", -1),
        passed_along(parts[2], "col", 1),
        passed_along(parts[3], "col", -1),
    ]


def body(rhs, smoother, blocks, col_index, send_list, agg_id, prolong, coarse_inverse):
    block_count = rhs.shape[2]
    dof_count = rhs.shape[3]
    vectors = rhs.shape[4]
    send_rows = send_list[0, 0]
    groups, ghost_count = send_rows.shape
    coarse_dofs = prolong.shape[2]
    shaped = prolong[0, 0].reshape((coarse_dofs, block_count, dof_count))
    local_blocks = blocks[0, 0]
    columns = col_index[0, 0]
    row_count = lax.axis_size("row")
    col_count = lax.axis_size("col")
    coarse_rows = coarse_inverse.shape[1] // (row_count * col_count)
    aggregates = coarse_rows // coarse_dofs
    onehot = (agg_id[0, 0][None, :] == jnp.arange(aggregates, dtype=jnp.int32)[:, None]).astype(
        jnp.float32
    )

    ghost_rows = ghost_count * dof_count

    def outgoing(vector):
        shard_low = vector.astype(jnp.bfloat16)[0, 0]
        packed = jnp.take(shard_low, send_rows.reshape(-1), axis=0)
        packed = packed.reshape((groups * ghost_rows, vectors))
        parts = [packed[g * ghost_rows:(g + 1) * ghost_rows] for g in range(groups)]
        return shard_low, parts

    def residual(prev, shard_low, ghosts):
        return block_product(local_blocks, columns, prev[0, 0], shard_low, ghosts, ghost_count)[
            None, None
        ]

    tables = []
    for g in range(groups):
        picked = jnp.take(shaped, send_rows[g], axis=1)
        member = jnp.take(onehot, send_rows[g], axis=1).astype(jnp.bfloat16)
        table = member.T[:, :, None, None] * jnp.transpose(picked, (1, 0, 2))[:, None, :, :]
        tables.append(table.reshape((ghost_count * coarse_rows * dof_count) // vectors, vectors))

    first_iter = point_smooth(smoother, rhs)
    shard_low, parts = outgoing(first_iter)
    residual_first = residual(rhs, shard_low, exchange(parts))
    update_second = point_smooth(smoother, residual_first)
    second_iter = first_iter + update_second
    shard_low, parts = outgoing(update_second)
    payloads = [jnp.concatenate([parts[g], tables[g]], axis=0) for g in range(groups)]
    arrived = exchange(payloads)
    neighbour_tables = [
        a[ghost_rows:].reshape((ghost_count, coarse_rows, dof_count)) for a in arrived
    ]
    residual_second = residual(residual_first, shard_low, arrived)
    local_terms = jnp.einsum(
        "knd,ndr->nkr",
        shaped,
        residual_second[0, 0].astype(jnp.bfloat16),
        preferred_element_type=jnp.float32,
    )
    coarse_residual = jnp.einsum(
        "an,nkr->akr", onehot, local_terms, precision=lax.Precision.HIGHEST
    )
    coarse_rhs = coarse_residual.astype(jnp.bfloat16).reshape((coarse_rows, vectors))
    column_part = gathered_copies(coarse_rhs, "row")
    held = coarse_inverse.reshape((coarse_inverse.shape[0], row_count, col_count, coarse_rows))
    held = lax.dynamic_slice_in_dim(held, lax.axis_index("col"), 1, 2)
    held = held.reshape((coarse_inverse.shape[0], row_count * coarse_rows))
    partial = jnp.dot(held, column_part, preferred_element_type=jnp.float32)
    partial = lax.all_to_all(partial, "col", 0, 0, tiled=True)
    coarse_solution = partial.reshape((col_count, coarse_rows, vectors)).sum(axis=0)
    coarse_flat = coarse_solution.astype(jnp.bfloat16)
    coarse_rounded = coarse_flat.reshape((aggregates, coarse_dofs, vectors))
    neighbour_coarse = exchange([coarse_flat] * groups)
    chosen = jnp.einsum(
        "an,akr->nkr",
        onehot.astype(jnp.bfloat16),
        coarse_rounded,
        preferred_element_type=jnp.float32,
    ).astype(jnp.bfloat16)
    correction = jnp.einsum("knd,nkr->ndr", shaped, chosen, preferred_element_type=jnp.float32)[
        None, None
    ]
    after_coarse = second_iter + correction
    ghost_corrections = [
        jnp.einsum(
            "bjd,jr->bdr", neighbour_tables[g], neighbour_coarse[g],
            preferred_element_type=jnp.float32,
        )
        .astype(jnp.bfloat16)
        .reshape((ghost_rows, vectors))
        for g in range(groups)
    ]
    correction_low = correction.astype(jnp.bfloat16)[0, 0]
    residual_third = residual(residual_second, correction_low, ghost_corrections)
    return after_coarse + point_smooth(smoother, residual_third)


def solution(mesh):
    placed = (
        P("row", "col", None, None, None),
        P("row", "col", None, None, None),
        P("row", "col", None, None, None),
        P("row", "col", None, None),
        P("row", "col", None, None),
        P("row", "col", None),
        P("row", "col", None, None),
        P("row", None),
    )
    return jax.shard_map(
        body,
        mesh=mesh,
        in_specs=placed,
        out_specs=P("row", "col", None, None, None),
        check_vma=False,
    )
```

```python
import functools

import jax
import jax.numpy as jnp
from jax import lax
from jax.experimental import pallas as pl
from jax.experimental.pallas import tpu as pltpu
from jax.sharding import PartitionSpec as P

damping = 0.6


def passed_along(value, axis, steps):
    count = lax.axis_size(axis)
    pairs = [(source, (source + steps) % count) for source in range(count)]
    return lax.ppermute(value, axis, pairs)


def point_smooth(coefficients, vector):
    leading = vector.shape[:2]
    blocks = vector.shape[2]
    grains = vector.shape[3] // 3
    columns = vector.shape[4]
    factors = coefficients.astype(jnp.float32).reshape(leading + (3, 3, blocks, grains))
    pieces = vector.reshape(leading + (blocks, 3, grains, columns))
    outputs = []
    for component in range(3):
        summed = factors[:, :, component, 0, :, :, None] * pieces[:, :, :, 0]
        summed = summed + factors[:, :, component, 1, :, :, None] * pieces[:, :, :, 1]
        summed = summed + factors[:, :, component, 2, :, :, None] * pieces[:, :, :, 2]
        outputs.append(summed)
    return damping * jnp.stack(outputs, axis=3).reshape(vector.shape)


def smoothed(factors_ref, j, vector):
    grains = vector.shape[0] // 3
    pieces = [vector[c * grains:(c + 1) * grains] for c in range(3)]
    outputs = []
    for component in range(3):
        weight = [factors_ref[j, component, c].astype(jnp.float32) for c in range(3)]
        summed = weight[0] * pieces[0]
        summed = summed + weight[1] * pieces[1]
        summed = summed + weight[2] * pieces[2]
        outputs.append(damping * summed)
    return jnp.concatenate(outputs, axis=0)


def product_kernel(stored, rows, mode, ghost_total, columns_ref, blocks_ref, prev_ref, local_ref, *rest):
    ghost_refs = rest[:ghost_total]
    rest = rest[ghost_total:]
    if mode == "plain":
        (out_ref, source, picked) = rest
    elif mode == "smooth":
        (factors_ref, base_ref, out_ref, next_ref, low_ref, source, picked) = rest
    else:
        (factors_ref, base_ref, out_ref, source, picked) = rest
    n = pl.program_id(0)
    block_count, dof = local_ref.shape[0], local_ref.shape[1]
    ghost_count = (source.shape[0] - block_count) // len(ghost_refs)

    @pl.when(n == 0)
    def _():
        source[0:block_count] = local_ref[...]
        for g, ref in enumerate(ghost_refs):
            for b in range(ghost_count):
                source[block_count + g * ghost_count + b] = ref[b * dof:(b + 1) * dof, :]

    for j in range(rows):
        for k in range(stored):
            picked[k * dof:(k + 1) * dof, :] = source[columns_ref[(n * rows + j) * stored + k]]
        left = prev_ref[j] - jnp.dot(blocks_ref[j], picked[...], preferred_element_type=jnp.float32)
        if mode == "plain":
            out_ref[j] = left
        elif mode == "smooth":
            out_ref[j] = left
            update = smoothed(factors_ref, j, left)
            next_ref[j] = base_ref[j] + update
            low_ref[j] = update.astype(low_ref.dtype)
        else:
            out_ref[j] = base_ref[j] + smoothed(factors_ref, j, left)


def block_product(blocks, columns, prev, local, ghosts, ghost_count, mode="plain", factors=None, base=None):
    block_count, dof, width = blocks.shape
    stored = width // dof
    vectors = local.shape[-1]
    rows = 6 if block_count % 6 == 0 else 1
    whole = lambda shape: pl.BlockSpec(shape, lambda n, c: (0,) * len(shape))
    tile = pl.BlockSpec((rows, dof, vectors), lambda n, c: (n, 0, 0))
    field = jax.ShapeDtypeStruct((block_count, dof, vectors), jnp.float32)
    in_specs = [
        pl.BlockSpec((rows, dof, width), lambda n, c: (n, 0, 0)),
        tile,
        whole(local.shape),
    ] + [whole(g.shape) for g in ghosts]
    operands = [blocks, prev, local] + list(ghosts)
    if mode != "plain":
        in_specs += [pl.BlockSpec((rows,) + factors.shape[1:], lambda n, c: (n, 0, 0, 0, 0)), tile]
        operands += [factors, base]
    if mode == "smooth":
        out_specs = [tile, tile, tile]
        out_shape = [field, field, jax.ShapeDtypeStruct(field.shape, jnp.bfloat16)]
    else:
        out_specs = tile
        out_shape = field
    grid_spec = pltpu.PrefetchScalarGridSpec(
        num_scalar_prefetch=1,
        grid=(block_count // rows,),
        in_specs=in_specs,
        out_specs=out_specs,
        scratch_shapes=[
            pltpu.VMEM((block_count + len(ghosts) * ghost_count, dof, vectors), local.dtype),
            pltpu.VMEM((width, vectors), local.dtype),
        ],
    )
    flops = 2 * block_count * dof * width * vectors
    moved = blocks.size * 2 + local.size * 2 * 3 + prev.size * 8 * (1 if mode == "plain" else 3)
    return pl.pallas_call(
        functools.partial(product_kernel, stored, rows, mode, len(ghosts)),
        grid_spec=grid_spec,
        out_shape=out_shape,
        cost_estimate=pl.CostEstimate(flops=flops, bytes_accessed=moved, transcendentals=0),
    )(columns.reshape(-1), *operands)


def gathered_copies(value, axis):
    count = lax.axis_size(axis)
    repeated = jnp.broadcast_to(value[None], (count,) + value.shape)
    repeated = repeated.reshape((count * value.shape[0],) + value.shape[1:])
    return lax.all_to_all(repeated, axis, 0, 0, tiled=True)


def exchange(parts):
    return [
        passed_along(parts[0], "row", 1),
        passed_along(parts[1], "row", -1),
        passed_along(parts[2], "col", 1),
        passed_along(parts[3], "col", -1),
    ]


def body(rhs, smoother, blocks, col_index, send_list, agg_id, prolong, coarse_inverse):
    block_count = rhs.shape[2]
    dof_count = rhs.shape[3]
    vectors = rhs.shape[4]
    send_rows = send_list[0, 0]
    groups, ghost_count = send_rows.shape
    coarse_dofs = prolong.shape[2]
    shaped = prolong[0, 0].reshape((coarse_dofs, block_count, dof_count))
    local_blocks = blocks[0, 0]
    columns = col_index[0, 0]
    row_count = lax.axis_size("row")
    col_count = lax.axis_size("col")
    coarse_rows = coarse_inverse.shape[1] // (row_count * col_count)
    aggregates = coarse_rows // coarse_dofs
    onehot = (agg_id[0, 0][None, :] == jnp.arange(aggregates, dtype=jnp.int32)[:, None]).astype(
        jnp.float32
    )

    ghost_rows = ghost_count * dof_count

    def outgoing(vector):
        shard_low = vector.astype(jnp.bfloat16)[0, 0]
        packed = jnp.take(shard_low, send_rows.reshape(-1), axis=0)
        packed = packed.reshape((groups * ghost_rows, vectors))
        parts = [packed[g * ghost_rows:(g + 1) * ghost_rows] for g in range(groups)]
        return shard_low, parts

    def residual(prev, shard_low, ghosts):
        return block_product(local_blocks, columns, prev[0, 0], shard_low, ghosts, ghost_count)[
            None, None
        ]

    grains = dof_count // 3
    factors = jnp.transpose(smoother[0, 0].reshape((3, 3, block_count, grains)), (2, 0, 1, 3))
    factors = jnp.broadcast_to(factors[..., None], factors.shape + (vectors,))

    tables = []
    for g in range(groups):
        picked = jnp.take(shaped, send_rows[g], axis=1)
        member = jnp.take(onehot, send_rows[g], axis=1).astype(jnp.bfloat16)
        table = member.T[:, :, None, None] * jnp.transpose(picked, (1, 0, 2))[:, None, :, :]
        tables.append(table.reshape((ghost_count * coarse_rows * dof_count) // vectors, vectors))

    first_iter = point_smooth(smoother, rhs)
    shard_low, parts = outgoing(first_iter)
    residual_first, second_iter, update_low = block_product(
        local_blocks, columns, rhs[0, 0], shard_low, exchange(parts), ghost_count,
        mode="smooth", factors=factors, base=first_iter[0, 0],
    )
    residual_first = residual_first[None, None]
    second_iter = second_iter[None, None]
    shard_low, parts = outgoing(update_low[None, None])
    payloads = [jnp.concatenate([parts[g], tables[g]], axis=0) for g in range(groups)]
    arrived = exchange(payloads)
    neighbour_tables = [
        a[ghost_rows:].reshape((ghost_count, coarse_rows, dof_count)) for a in arrived
    ]
    residual_second = residual(residual_first, shard_low, arrived)
    local_terms = jnp.einsum(
        "knd,ndr->nkr",
        shaped,
        residual_second[0, 0].astype(jnp.bfloat16),
        preferred_element_type=jnp.float32,
    )
    coarse_residual = jnp.einsum(
        "an,nkr->akr", onehot, local_terms, precision=lax.Precision.HIGHEST
    )
    coarse_rhs = coarse_residual.astype(jnp.bfloat16).reshape((coarse_rows, vectors))
    column_part = gathered_copies(coarse_rhs, "row")
    held = coarse_inverse.reshape((coarse_inverse.shape[0], row_count, col_count, coarse_rows))
    held = lax.dynamic_slice_in_dim(held, lax.axis_index("col"), 1, 2)
    held = held.reshape((coarse_inverse.shape[0], row_count * coarse_rows))
    partial = jnp.dot(held, column_part, preferred_element_type=jnp.float32)
    partial = lax.all_to_all(partial, "col", 0, 0, tiled=True)
    coarse_solution = partial.reshape((col_count, coarse_rows, vectors)).sum(axis=0)
    coarse_flat = coarse_solution.astype(jnp.bfloat16)
    coarse_rounded = coarse_flat.reshape((aggregates, coarse_dofs, vectors))
    neighbour_coarse = exchange([coarse_flat] * groups)
    chosen = jnp.einsum(
        "an,akr->nkr",
        onehot.astype(jnp.bfloat16),
        coarse_rounded,
        preferred_element_type=jnp.float32,
    ).astype(jnp.bfloat16)
    correction = jnp.einsum("knd,nkr->ndr", shaped, chosen, preferred_element_type=jnp.float32)[
        None, None
    ]
    after_coarse = second_iter + correction
    ghost_corrections = [
        jnp.einsum(
            "bjd,jr->bdr", neighbour_tables[g], neighbour_coarse[g],
            preferred_element_type=jnp.float32,
        )
        .astype(jnp.bfloat16)
        .reshape((ghost_rows, vectors))
        for g in range(groups)
    ]
    correction_low = correction.astype(jnp.bfloat16)[0, 0]
    smoothed_solution = block_product(
        local_blocks, columns, residual_second[0, 0], correction_low, ghost_corrections,
        ghost_count, mode="final", factors=factors, base=after_coarse[0, 0],
    )
    return smoothed_solution[None, None]


def solution(mesh):
    placed = (
        P("row", "col", None, None, None),
        P("row", "col", None, None, None),
        P("row", "col", None, None, None),
        P("row", "col", None, None),
        P("row", "col", None, None),
        P("row", "col", None),
        P("row", "col", None, None),
        P("row", None),
    )
    return jax.shard_map(
        body,
        mesh=mesh,
        in_specs=placed,
        out_specs=P("row", "col", None, None, None),
        check_vma=False,
    )
```

```python
import functools

import jax
import jax.numpy as jnp
from jax import lax
from jax.experimental import pallas as pl
from jax.experimental.pallas import tpu as pltpu
from jax.sharding import PartitionSpec as P


damping = 0.6


def passed_along(value, axis, steps):
    count = lax.axis_size(axis)
    pairs = [(source, (source + steps) % count) for source in range(count)]
    return lax.ppermute(value, axis, pairs)


def point_smooth(coefficients, vector):
    leading = vector.shape[:2]
    blocks = vector.shape[2]
    grains = vector.shape[3] // 3
    columns = vector.shape[4]
    factors = coefficients.astype(jnp.float32).reshape(leading + (3, 3, blocks, grains))
    pieces = vector.reshape(leading + (blocks, 3, grains, columns))
    outputs = []
    for component in range(3):
        summed = factors[:, :, component, 0, :, :, None] * pieces[:, :, :, 0]
        summed = summed + factors[:, :, component, 1, :, :, None] * pieces[:, :, :, 1]
        summed = summed + factors[:, :, component, 2, :, :, None] * pieces[:, :, :, 2]
        outputs.append(summed)
    return damping * jnp.stack(outputs, axis=3).reshape(vector.shape)


def smoothed(factors_ref, j, vector):
    grains = vector.shape[0] // 3
    pieces = [vector[c * grains:(c + 1) * grains] for c in range(3)]
    outputs = []
    for component in range(3):
        weight = [factors_ref[j, component, c].astype(jnp.float32) for c in range(3)]
        summed = weight[0] * pieces[0]
        summed = summed + weight[1] * pieces[1]
        summed = summed + weight[2] * pieces[2]
        outputs.append(damping * summed)
    return jnp.concatenate(outputs, axis=0)


def product_kernel(stored, rows, mode, ghost_total, columns_ref, blocks_ref, prev_ref, local_ref, *rest):
    ghost_refs = rest[:ghost_total]
    rest = rest[ghost_total:]
    if mode == "plain":
        (out_ref, source, picked) = rest
    elif mode == "smooth":
        (factors_ref, base_ref, out_ref, next_ref, low_ref, source, picked) = rest
    else:
        (factors_ref, base_ref, out_ref, source, picked) = rest
    n = pl.program_id(0)
    block_count, dof = local_ref.shape[0], local_ref.shape[1]
    ghost_count = (source.shape[0] - block_count) // len(ghost_refs)

    @pl.when(n == 0)
    def _():
        source[0:block_count] = local_ref[...]
        for g, ref in enumerate(ghost_refs):
            for b in range(ghost_count):
                source[block_count + g * ghost_count + b] = ref[b * dof:(b + 1) * dof, :]

    for j in range(rows):
        for k in range(stored):
            picked[k * dof:(k + 1) * dof, :] = source[columns_ref[(n * rows + j) * stored + k]]
        left = prev_ref[j] - jnp.dot(blocks_ref[j], picked[...], preferred_element_type=jnp.float32)
        if mode == "plain":
            out_ref[j] = left
        elif mode == "smooth":
            out_ref[j] = left
            update = smoothed(factors_ref, j, left)
            next_ref[j] = base_ref[j] + update
            low_ref[j] = update.astype(low_ref.dtype)
        else:
            out_ref[j] = base_ref[j] + smoothed(factors_ref, j, left)


def block_product(blocks, columns, prev, local, ghosts, ghost_count, mode="plain", factors=None, base=None):
    block_count, dof, width = blocks.shape
    stored = width // dof
    vectors = local.shape[-1]
    rows = 6 if block_count % 6 == 0 else 1
    whole = lambda shape: pl.BlockSpec(shape, lambda n, c: (0,) * len(shape))
    tile = pl.BlockSpec((rows, dof, vectors), lambda n, c: (n, 0, 0))
    field = jax.ShapeDtypeStruct((block_count, dof, vectors), jnp.float32)
    in_specs = [
        pl.BlockSpec((rows, dof, width), lambda n, c: (n, 0, 0)),
        tile,
        whole(local.shape),
    ] + [whole(g.shape) for g in ghosts]
    operands = [blocks, prev, local] + list(ghosts)
    if mode != "plain":
        in_specs += [pl.BlockSpec((rows,) + factors.shape[1:], lambda n, c: (n, 0, 0, 0, 0)), tile]
        operands += [factors, base]
    if mode == "smooth":
        out_specs = [tile, tile, tile]
        out_shape = [field, field, jax.ShapeDtypeStruct(field.shape, jnp.bfloat16)]
    else:
        out_specs = tile
        out_shape = field
    grid_spec = pltpu.PrefetchScalarGridSpec(
        num_scalar_prefetch=1,
        grid=(block_count // rows,),
        in_specs=in_specs,
        out_specs=out_specs,
        scratch_shapes=[
            pltpu.VMEM((block_count + len(ghosts) * ghost_count, dof, vectors), local.dtype),
            pltpu.VMEM((width, vectors), local.dtype),
        ],
    )
    flops = 2 * block_count * dof * width * vectors
    moved = blocks.size * 2 + local.size * 2 * 3 + prev.size * 8 * (1 if mode == "plain" else 3)
    return pl.pallas_call(
        functools.partial(product_kernel, stored, rows, mode, len(ghosts)),
        grid_spec=grid_spec,
        out_shape=out_shape,
        cost_estimate=pl.CostEstimate(flops=flops, bytes_accessed=moved, transcendentals=0),
    )(columns.reshape(-1), *operands)


def gathered_copies(value, axis):
    count = lax.axis_size(axis)
    repeated = jnp.broadcast_to(value[None], (count,) + value.shape)
    repeated = repeated.reshape((count * value.shape[0],) + value.shape[1:])
    return lax.all_to_all(repeated, axis, 0, 0, tiled=True)


def exchange(parts):
    return [
        passed_along(parts[0], "row", 1),
        passed_along(parts[1], "row", -1),
        passed_along(parts[2], "col", 1),
        passed_along(parts[3], "col", -1),
    ]


def cycle(rhs, smoother, blocks, col_index, send_list, agg_id, prolong, coarse_inverse):
    block_count = rhs.shape[2]
    dof_count = rhs.shape[3]
    vectors = rhs.shape[4]
    send_rows = send_list[0, 0]
    groups, ghost_count = send_rows.shape
    coarse_dofs = prolong.shape[2]
    shaped = prolong[0, 0].reshape((coarse_dofs, block_count, dof_count))
    local_blocks = blocks[0, 0]
    columns = col_index[0, 0]
    row_count = lax.axis_size("row")
    col_count = lax.axis_size("col")
    coarse_rows = coarse_inverse.shape[1] // (row_count * col_count)
    aggregates = coarse_rows // coarse_dofs
    onehot = (agg_id[0, 0][None, :] == jnp.arange(aggregates, dtype=jnp.int32)[:, None]).astype(
        jnp.float32
    )

    ghost_rows = ghost_count * dof_count

    def outgoing(vector):
        shard_low = vector.astype(jnp.bfloat16)[0, 0]
        packed = jnp.take(shard_low, send_rows.reshape(-1), axis=0)
        packed = packed.reshape((groups * ghost_rows, vectors))
        parts = [packed[g * ghost_rows:(g + 1) * ghost_rows] for g in range(groups)]
        return shard_low, parts

    def residual(prev, shard_low, ghosts):
        return block_product(local_blocks, columns, prev[0, 0], shard_low, ghosts, ghost_count)[
            None, None
        ]

    grains = dof_count // 3
    factors = jnp.transpose(
        smoother[0, 0].reshape((3, 3, block_count, grains)), (2, 0, 1, 3)
    )
    factors = jnp.broadcast_to(factors[..., None], factors.shape + (vectors,))

    tables = []
    for g in range(groups):
        picked = jnp.take(shaped, send_rows[g], axis=1)
        member = jnp.take(onehot, send_rows[g], axis=1).astype(jnp.bfloat16)
        table = member.T[:, :, None, None] * jnp.transpose(picked, (1, 0, 2))[:, None, :, :]
        tables.append(table.reshape((ghost_count * coarse_rows * dof_count) // vectors, vectors))

    sent = send_rows.reshape(-1)
    sent_rhs = jnp.take(rhs, sent, axis=2)
    sent_factors = jnp.take(
        smoother.reshape(smoother.shape[:4] + (block_count, grains)), sent, axis=4
    ).reshape(smoother.shape[:4] + (sent.shape[0] * grains,))
    sent_low = point_smooth(sent_factors, sent_rhs).astype(jnp.bfloat16)[0, 0]
    sent_low = sent_low.reshape((groups * ghost_rows, vectors))
    parts = [sent_low[g * ghost_rows:(g + 1) * ghost_rows] for g in range(groups)]
    first_ghosts = exchange(parts)
    first_iter = point_smooth(smoother, rhs)
    shard_low = first_iter.astype(jnp.bfloat16)[0, 0]
    residual_first, second_iter, update_low = block_product(
        local_blocks, columns, rhs[0, 0], shard_low, first_ghosts, ghost_count,
        mode="smooth", factors=factors, base=first_iter[0, 0],
    )
    residual_first = residual_first[None, None]
    second_iter = second_iter[None, None]
    shard_low, parts = outgoing(update_low[None, None])
    payloads = [jnp.concatenate([parts[g], tables[g]], axis=0) for g in range(groups)]
    arrived = exchange(payloads)
    neighbour_tables = [
        a[ghost_rows:].reshape((ghost_count, coarse_rows, dof_count)) for a in arrived
    ]
    residual_second = residual(residual_first, shard_low, arrived)
    local_terms = jnp.einsum(
        "knd,ndr->nkr",
        shaped,
        residual_second[0, 0].astype(jnp.bfloat16),
        preferred_element_type=jnp.float32,
    )
    coarse_residual = jnp.einsum(
        "an,nkr->akr", onehot, local_terms, precision=lax.Precision.HIGHEST
    )
    coarse_rhs = coarse_residual.astype(jnp.bfloat16).reshape((coarse_rows, vectors))
    column_part = gathered_copies(coarse_rhs, "row")
    held = coarse_inverse.reshape((coarse_inverse.shape[0], row_count, col_count, coarse_rows))
    held = lax.dynamic_slice_in_dim(held, lax.axis_index("col"), 1, 2)
    held = held.reshape((coarse_inverse.shape[0], row_count * coarse_rows))
    partial = jnp.dot(held, column_part, preferred_element_type=jnp.float32)
    partial = lax.all_to_all(partial, "col", 0, 0, tiled=True)
    coarse_solution = partial.reshape((col_count, coarse_rows, vectors)).sum(axis=0)
    coarse_flat = coarse_solution.astype(jnp.bfloat16)
    coarse_rounded = coarse_flat.reshape((aggregates, coarse_dofs, vectors))
    neighbour_coarse = exchange([coarse_flat] * groups)
    chosen = jnp.einsum(
        "an,akr->nkr",
        onehot.astype(jnp.bfloat16),
        coarse_rounded,
        preferred_element_type=jnp.float32,
    ).astype(jnp.bfloat16)
    correction = jnp.einsum("knd,nkr->ndr", shaped, chosen, preferred_element_type=jnp.float32)[
        None, None
    ]
    after_coarse = second_iter + correction
    ghost_corrections = [
        jnp.einsum(
            "bjd,jr->bdr", neighbour_tables[g], neighbour_coarse[g],
            preferred_element_type=jnp.float32,
        )
        .astype(jnp.bfloat16)
        .reshape((ghost_rows, vectors))
        for g in range(groups)
    ]
    correction_low = correction.astype(jnp.bfloat16)[0, 0]
    smoothed_solution = block_product(
        local_blocks, columns, residual_second[0, 0], correction_low, ghost_corrections,
        ghost_count, mode="final", factors=factors, base=after_coarse[0, 0],
    )
    return smoothed_solution[None, None]


def solution(mesh):
    placed = (
        P("row", "col", None, None, None),
        P("row", "col", None, None, None),
        P("row", "col", None, None, None),
        P("row", "col", None, None),
        P("row", "col", None, None),
        P("row", "col", None),
        P("row", "col", None, None),
        P("row", None),
    )
    return jax.shard_map(
        cycle,
        mesh=mesh,
        in_specs=placed,
        out_specs=P("row", "col", None, None, None),
        check_vma=False,
    )
```

```python
import functools

import jax
import jax.numpy as jnp
from jax import lax
from jax.experimental import pallas as pl
from jax.experimental.pallas import tpu as pltpu
from jax.sharding import PartitionSpec as P


damping = 0.6


def passed_along(value, axis, steps):
    count = lax.axis_size(axis)
    pairs = [(source, (source + steps) % count) for source in range(count)]
    return lax.ppermute(value, axis, pairs)


def point_smooth(coefficients, vector):
    leading = vector.shape[:2]
    blocks = vector.shape[2]
    grains = vector.shape[3] // 3
    columns = vector.shape[4]
    factors = coefficients.astype(jnp.float32).reshape(leading + (3, 3, blocks, grains))
    pieces = vector.reshape(leading + (blocks, 3, grains, columns))
    outputs = []
    for component in range(3):
        summed = factors[:, :, component, 0, :, :, None] * pieces[:, :, :, 0]
        summed = summed + factors[:, :, component, 1, :, :, None] * pieces[:, :, :, 1]
        summed = summed + factors[:, :, component, 2, :, :, None] * pieces[:, :, :, 2]
        outputs.append(summed)
    return damping * jnp.stack(outputs, axis=3).reshape(vector.shape)


def smoothed(factors_ref, j, vector):
    grains = vector.shape[0] // 3
    pieces = [vector[c * grains:(c + 1) * grains] for c in range(3)]
    outputs = []
    for component in range(3):
        weight = [factors_ref[j, component, c].astype(jnp.float32) for c in range(3)]
        summed = weight[0] * pieces[0]
        summed = summed + weight[1] * pieces[1]
        summed = summed + weight[2] * pieces[2]
        outputs.append(damping * summed)
    return jnp.concatenate(outputs, axis=0)


def product_kernel(
    stored, rows, mode, ghost_total, columns_ref, send_ref, blocks_ref, prev_ref, local_ref, *rest
):
    ghost_refs = rest[:ghost_total]
    rest = rest[ghost_total:]
    if mode == "plain":
        (out_ref, source, picked) = rest
    elif mode == "smooth":
        (factors_ref, base_ref, out_ref, next_ref, low_ref, sends_ref, source, picked, kept) = rest
    else:
        (factors_ref, base_ref, out_ref, source, picked) = rest
    n = pl.program_id(0)
    block_count, dof = local_ref.shape[0], local_ref.shape[1]
    ghost_count = (source.shape[0] - block_count) // len(ghost_refs)

    @pl.when(n == 0)
    def _():
        source[0:block_count] = local_ref[...]
        for g, ref in enumerate(ghost_refs):
            for b in range(ghost_count):
                source[block_count + g * ghost_count + b] = ref[b * dof:(b + 1) * dof, :]

    for j in range(rows):
        for k in range(stored):
            picked[k * dof:(k + 1) * dof, :] = source[columns_ref[(n * rows + j) * stored + k]]
        left = prev_ref[j] - jnp.dot(blocks_ref[j], picked[...], preferred_element_type=jnp.float32)
        if mode == "plain":
            out_ref[j] = left
        elif mode == "smooth":
            out_ref[j] = left
            update = smoothed(factors_ref, j, left)
            next_ref[j] = base_ref[j] + update
            low = update.astype(low_ref.dtype)
            low_ref[j] = low
            kept[n * rows + j] = low
        else:
            out_ref[j] = base_ref[j] + smoothed(factors_ref, j, left)

    if mode == "smooth":

        @pl.when(n == pl.num_programs(0) - 1)
        def _():
            for i in range(sends_ref.shape[0] // dof):
                sends_ref[i * dof:(i + 1) * dof, :] = kept[send_ref[i]]


def block_product(
    blocks, columns, prev, local, ghosts, ghost_count, mode="plain", factors=None, base=None,
    send=None,
):
    block_count, dof, width = blocks.shape
    stored = width // dof
    vectors = local.shape[-1]
    rows = 6 if block_count % 6 == 0 else 1
    whole = lambda shape: pl.BlockSpec(shape, lambda n, c, s: (0,) * len(shape))
    tile = pl.BlockSpec((rows, dof, vectors), lambda n, c, s: (n, 0, 0))
    field = jax.ShapeDtypeStruct((block_count, dof, vectors), jnp.float32)
    in_specs = [
        pl.BlockSpec((rows, dof, width), lambda n, c, s: (n, 0, 0)),
        tile,
        whole(local.shape),
    ] + [whole(g.shape) for g in ghosts]
    operands = [blocks, prev, local] + list(ghosts)
    if mode != "plain":
        in_specs += [pl.BlockSpec((rows,) + factors.shape[1:], lambda n, c, s: (n, 0, 0, 0, 0)), tile]
        operands += [factors, base]
    scratch = [
        pltpu.VMEM((block_count + len(ghosts) * ghost_count, dof, vectors), local.dtype),
        pltpu.VMEM((width, vectors), local.dtype),
    ]
    if send is None:
        send = jnp.zeros((1,), jnp.int32)
    if mode == "smooth":
        sends_shape = (send.shape[0] * dof, vectors)
        out_specs = [tile, tile, tile, whole(sends_shape)]
        out_shape = [
            field,
            field,
            jax.ShapeDtypeStruct(field.shape, jnp.bfloat16),
            jax.ShapeDtypeStruct(sends_shape, jnp.bfloat16),
        ]
        scratch.append(pltpu.VMEM((block_count, dof, vectors), jnp.bfloat16))
    else:
        out_specs = tile
        out_shape = field
    grid_spec = pltpu.PrefetchScalarGridSpec(
        num_scalar_prefetch=2,
        grid=(block_count // rows,),
        in_specs=in_specs,
        out_specs=out_specs,
        scratch_shapes=scratch,
    )
    flops = 2 * block_count * dof * width * vectors
    moved = blocks.size * 2 + local.size * 2 * 3 + prev.size * 8 * (1 if mode == "plain" else 3)
    return pl.pallas_call(
        functools.partial(product_kernel, stored, rows, mode, len(ghosts)),
        grid_spec=grid_spec,
        out_shape=out_shape,
        cost_estimate=pl.CostEstimate(flops=flops, bytes_accessed=moved, transcendentals=0),
    )(columns.reshape(-1), send, *operands)


def gathered_copies(value, axis):
    count = lax.axis_size(axis)
    repeated = jnp.broadcast_to(value[None], (count,) + value.shape)
    repeated = repeated.reshape((count * value.shape[0],) + value.shape[1:])
    return lax.all_to_all(repeated, axis, 0, 0, tiled=True)


def exchange(parts):
    return [
        passed_along(parts[0], "row", 1),
        passed_along(parts[1], "row", -1),
        passed_along(parts[2], "col", 1),
        passed_along(parts[3], "col", -1),
    ]


def cycle(rhs, smoother, blocks, col_index, send_list, agg_id, prolong, coarse_inverse):
    block_count = rhs.shape[2]
    dof_count = rhs.shape[3]
    vectors = rhs.shape[4]
    send_rows = send_list[0, 0]
    groups, ghost_count = send_rows.shape
    coarse_dofs = prolong.shape[2]
    shaped = prolong[0, 0].reshape((coarse_dofs, block_count, dof_count))
    local_blocks = blocks[0, 0]
    columns = col_index[0, 0]
    row_count = lax.axis_size("row")
    col_count = lax.axis_size("col")
    coarse_rows = coarse_inverse.shape[1] // (row_count * col_count)
    aggregates = coarse_rows // coarse_dofs
    onehot = (agg_id[0, 0][None, :] == jnp.arange(aggregates, dtype=jnp.int32)[:, None]).astype(
        jnp.float32
    )

    ghost_rows = ghost_count * dof_count

    def residual(prev, shard_low, ghosts):
        return block_product(local_blocks, columns, prev[0, 0], shard_low, ghosts, ghost_count)[
            None, None
        ]

    grains = dof_count // 3
    factors = jnp.transpose(
        smoother[0, 0].reshape((3, 3, block_count, grains)), (2, 0, 1, 3)
    )
    factors = jnp.broadcast_to(factors[..., None], factors.shape + (vectors,))

    tables = []
    for g in range(groups):
        picked = jnp.take(shaped, send_rows[g], axis=1)
        member = jnp.take(onehot, send_rows[g], axis=1).astype(jnp.bfloat16)
        table = member.T[:, :, None, None] * jnp.transpose(picked, (1, 0, 2))[:, None, :, :]
        tables.append(table.reshape((ghost_count * coarse_rows * dof_count) // vectors, vectors))

    sent = send_rows.reshape(-1)
    sent_rhs = jnp.take(rhs, sent, axis=2)
    sent_factors = jnp.take(
        smoother.reshape(smoother.shape[:4] + (block_count, grains)), sent, axis=4
    ).reshape(smoother.shape[:4] + (sent.shape[0] * grains,))
    sent_low = point_smooth(sent_factors, sent_rhs).astype(jnp.bfloat16)[0, 0]
    sent_low = sent_low.reshape((groups * ghost_rows, vectors))
    parts = [sent_low[g * ghost_rows:(g + 1) * ghost_rows] for g in range(groups)]
    first_ghosts = exchange(parts)
    first_iter = point_smooth(smoother, rhs)
    shard_low = first_iter.astype(jnp.bfloat16)[0, 0]
    residual_first, second_iter, shard_low, packed = block_product(
        local_blocks, columns, rhs[0, 0], shard_low, first_ghosts, ghost_count,
        mode="smooth", factors=factors, base=first_iter[0, 0], send=sent,
    )
    residual_first = residual_first[None, None]
    second_iter = second_iter[None, None]
    parts = [packed[g * ghost_rows:(g + 1) * ghost_rows] for g in range(groups)]
    payloads = [jnp.concatenate([parts[g], tables[g]], axis=0) for g in range(groups)]
    arrived = exchange(payloads)
    neighbour_tables = [
        a[ghost_rows:].reshape((ghost_count, coarse_rows, dof_count)) for a in arrived
    ]
    residual_second = residual(residual_first, shard_low, arrived)
    local_terms = jnp.einsum(
        "knd,ndr->nkr",
        shaped,
        residual_second[0, 0].astype(jnp.bfloat16),
        preferred_element_type=jnp.float32,
    )
    coarse_residual = jnp.einsum(
        "an,nkr->akr", onehot, local_terms, precision=lax.Precision.HIGHEST
    )
    coarse_rhs = coarse_residual.astype(jnp.bfloat16).reshape((coarse_rows, vectors))
    column_part = gathered_copies(coarse_rhs, "row")
    held = coarse_inverse.reshape((coarse_inverse.shape[0], row_count, col_count, coarse_rows))
    held = lax.dynamic_slice_in_dim(held, lax.axis_index("col"), 1, 2)
    held = held.reshape((coarse_inverse.shape[0], row_count * coarse_rows))
    partial = jnp.dot(held, column_part, preferred_element_type=jnp.float32)
    partial = partial.reshape((col_count, coarse_rows, vectors))
    places = jnp.arange(col_count, dtype=jnp.int32)
    around = jnp.stack([(places - 1) % col_count, places, (places + 1) % col_count], axis=1)
    partial = jnp.take(partial, around.reshape(-1), axis=0)
    partial = partial.reshape((col_count, 3, coarse_rows, vectors))
    partial = lax.all_to_all(partial, "col", 0, 0, tiled=True)
    coarse_solution = partial.sum(axis=0).astype(jnp.bfloat16)
    coarse_flat = coarse_solution[1]
    coarse_rounded = coarse_flat.reshape((aggregates, coarse_dofs, vectors))
    neighbour_coarse = [
        passed_along(coarse_flat, "row", 1),
        passed_along(coarse_flat, "row", -1),
        coarse_solution[0],
        coarse_solution[2],
    ]
    chosen = jnp.einsum(
        "an,akr->nkr",
        onehot.astype(jnp.bfloat16),
        coarse_rounded,
        preferred_element_type=jnp.float32,
    ).astype(jnp.bfloat16)
    correction = jnp.einsum("knd,nkr->ndr", shaped, chosen, preferred_element_type=jnp.float32)[
        None, None
    ]
    after_coarse = second_iter + correction
    ghost_corrections = [
        jnp.einsum(
            "bjd,jr->bdr", neighbour_tables[g], neighbour_coarse[g],
            preferred_element_type=jnp.float32,
        )
        .astype(jnp.bfloat16)
        .reshape((ghost_rows, vectors))
        for g in range(groups)
    ]
    correction_low = correction.astype(jnp.bfloat16)[0, 0]
    smoothed_solution = block_product(
        local_blocks, columns, residual_second[0, 0], correction_low, ghost_corrections,
        ghost_count, mode="final", factors=factors, base=after_coarse[0, 0],
    )
    return smoothed_solution[None, None]


def solution(mesh):
    placed = (
        P("row", "col", None, None, None),
        P("row", "col", None, None, None),
        P("row", "col", None, None, None),
        P("row", "col", None, None),
        P("row", "col", None, None),
        P("row", "col", None),
        P("row", "col", None, None),
        P("row", None),
    )
    return jax.shard_map(
        cycle,
        mesh=mesh,
        in_specs=placed,
        out_specs=P("row", "col", None, None, None),
        check_vma=False,
    )
```

```python
import functools

import jax
import jax.numpy as jnp
from jax import lax
from jax.experimental import pallas as pl
from jax.experimental.pallas import tpu as pltpu
from jax.sharding import PartitionSpec as P


damping = 0.6


def passed_along(value, axis, steps):
    count = lax.axis_size(axis)
    pairs = [(source, (source + steps) % count) for source in range(count)]
    return lax.ppermute(value, axis, pairs)


def point_smooth(coefficients, vector):
    leading = vector.shape[:2]
    blocks = vector.shape[2]
    grains = vector.shape[3] // 3
    columns = vector.shape[4]
    factors = coefficients.astype(jnp.float32).reshape(leading + (3, 3, blocks, grains))
    pieces = vector.reshape(leading + (blocks, 3, grains, columns))
    outputs = []
    for component in range(3):
        summed = factors[:, :, component, 0, :, :, None] * pieces[:, :, :, 0]
        summed = summed + factors[:, :, component, 1, :, :, None] * pieces[:, :, :, 1]
        summed = summed + factors[:, :, component, 2, :, :, None] * pieces[:, :, :, 2]
        outputs.append(summed)
    return damping * jnp.stack(outputs, axis=3).reshape(vector.shape)


def smoothed(factors_ref, j, vector):
    grains = vector.shape[0] // 3
    pieces = [vector[c * grains:(c + 1) * grains] for c in range(3)]
    outputs = []
    for component in range(3):
        weight = [factors_ref[j, component, c].astype(jnp.float32) for c in range(3)]
        summed = weight[0] * pieces[0]
        summed = summed + weight[1] * pieces[1]
        summed = summed + weight[2] * pieces[2]
        outputs.append(damping * summed)
    return jnp.concatenate(outputs, axis=0)


def product_kernel(
    stored, rows, mode, ghost_total, columns_ref, send_ref, blocks_ref, prev_ref, local_ref, *rest
):
    ghost_refs = rest[:ghost_total]
    rest = rest[ghost_total:]
    if mode == "plain":
        (out_ref, source, picked) = rest
    elif mode == "smooth":
        (factors_ref, base_ref) = rest[:2]
        table_refs = rest[2:2 + ghost_total]
        (out_ref, next_ref, low_ref) = rest[2 + ghost_total:5 + ghost_total]
        payload_refs = rest[5 + ghost_total:5 + 2 * ghost_total]
        (source, picked, kept) = rest[5 + 2 * ghost_total:]
    else:
        (factors_ref, base_ref, out_ref, source, picked) = rest
    n = pl.program_id(0)
    block_count, dof = local_ref.shape[0], local_ref.shape[1]
    ghost_count = (source.shape[0] - block_count) // len(ghost_refs)

    @pl.when(n == 0)
    def _():
        source[0:block_count] = local_ref[...]
        for g, ref in enumerate(ghost_refs):
            for b in range(ghost_count):
                source[block_count + g * ghost_count + b] = ref[b * dof:(b + 1) * dof, :]

    for j in range(rows):
        for k in range(stored):
            picked[k * dof:(k + 1) * dof, :] = source[columns_ref[(n * rows + j) * stored + k]]
        left = prev_ref[j] - jnp.dot(blocks_ref[j], picked[...], preferred_element_type=jnp.float32)
        if mode == "plain":
            out_ref[j] = left
        elif mode == "smooth":
            out_ref[j] = left
            update = smoothed(factors_ref, j, left)
            next_ref[j] = base_ref[j] + update
            low = update.astype(low_ref.dtype)
            low_ref[j] = low
            kept[n * rows + j] = low
        else:
            out_ref[j] = base_ref[j] + smoothed(factors_ref, j, left)

    if mode == "smooth":

        @pl.when(n == pl.num_programs(0) - 1)
        def _():
            for g, ref in enumerate(payload_refs):
                for b in range(ghost_count):
                    ref[b * dof:(b + 1) * dof, :] = kept[send_ref[g * ghost_count + b]]
                ref[ghost_count * dof:, :] = table_refs[g][...]


def block_product(
    blocks, columns, prev, local, ghosts, ghost_count, mode="plain", factors=None, base=None,
    send=None, tables=(),
):
    block_count, dof, width = blocks.shape
    stored = width // dof
    vectors = local.shape[-1]
    rows = 6 if block_count % 6 == 0 else 1
    whole = lambda shape: pl.BlockSpec(shape, lambda n, c, s: (0,) * len(shape))
    tile = pl.BlockSpec((rows, dof, vectors), lambda n, c, s: (n, 0, 0))
    field = jax.ShapeDtypeStruct((block_count, dof, vectors), jnp.float32)
    in_specs = [
        pl.BlockSpec((rows, dof, width), lambda n, c, s: (n, 0, 0)),
        tile,
        whole(local.shape),
    ] + [whole(g.shape) for g in ghosts]
    operands = [blocks, prev, local] + list(ghosts)
    if mode != "plain":
        in_specs += [pl.BlockSpec((rows,) + factors.shape[1:], lambda n, c, s: (n, 0, 0, 0, 0)), tile]
        operands += [factors, base]
    if mode == "smooth":
        in_specs += [whole(t.shape) for t in tables]
        operands += list(tables)
    scratch = [
        pltpu.VMEM((block_count + len(ghosts) * ghost_count, dof, vectors), local.dtype),
        pltpu.VMEM((width, vectors), local.dtype),
    ]
    if send is None:
        send = jnp.zeros((1,), jnp.int32)
    if mode == "smooth":
        payload = [(ghost_count * dof + t.shape[0], vectors) for t in tables]
        out_specs = [tile, tile, tile] + [whole(p) for p in payload]
        out_shape = [
            field,
            field,
            jax.ShapeDtypeStruct(field.shape, jnp.bfloat16),
        ] + [jax.ShapeDtypeStruct(p, jnp.bfloat16) for p in payload]
        scratch.append(pltpu.VMEM((block_count, dof, vectors), jnp.bfloat16))
    else:
        out_specs = tile
        out_shape = field
    grid_spec = pltpu.PrefetchScalarGridSpec(
        num_scalar_prefetch=2,
        grid=(block_count // rows,),
        in_specs=in_specs,
        out_specs=out_specs,
        scratch_shapes=scratch,
    )
    flops = 2 * block_count * dof * width * vectors
    moved = blocks.size * 2 + local.size * 2 * 3 + prev.size * 8 * (1 if mode == "plain" else 3)
    return pl.pallas_call(
        functools.partial(product_kernel, stored, rows, mode, len(ghosts)),
        grid_spec=grid_spec,
        out_shape=out_shape,
        cost_estimate=pl.CostEstimate(flops=flops, bytes_accessed=moved, transcendentals=0),
    )(columns.reshape(-1), send, *operands)


def gathered_copies(value, axis):
    count = lax.axis_size(axis)
    repeated = jnp.broadcast_to(value[None], (count,) + value.shape)
    repeated = repeated.reshape((count * value.shape[0],) + value.shape[1:])
    return lax.all_to_all(repeated, axis, 0, 0, tiled=True)


def exchange(parts):
    return [
        passed_along(parts[0], "row", 1),
        passed_along(parts[1], "row", -1),
        passed_along(parts[2], "col", 1),
        passed_along(parts[3], "col", -1),
    ]


def cycle(rhs, smoother, blocks, col_index, send_list, agg_id, prolong, coarse_inverse):
    block_count = rhs.shape[2]
    dof_count = rhs.shape[3]
    vectors = rhs.shape[4]
    send_rows = send_list[0, 0]
    groups, ghost_count = send_rows.shape
    coarse_dofs = prolong.shape[2]
    shaped = prolong[0, 0].reshape((coarse_dofs, block_count, dof_count))
    local_blocks = blocks[0, 0]
    columns = col_index[0, 0]
    row_count = lax.axis_size("row")
    col_count = lax.axis_size("col")
    coarse_rows = coarse_inverse.shape[1] // (row_count * col_count)
    aggregates = coarse_rows // coarse_dofs
    onehot = (agg_id[0, 0][None, :] == jnp.arange(aggregates, dtype=jnp.int32)[:, None]).astype(
        jnp.float32
    )

    ghost_rows = ghost_count * dof_count

    def outgoing(vector):
        shard_low = vector.astype(jnp.bfloat16)[0, 0]
        packed = jnp.take(shard_low, send_rows.reshape(-1), axis=0)
        packed = packed.reshape((groups * ghost_rows, vectors))
        parts = [packed[g * ghost_rows:(g + 1) * ghost_rows] for g in range(groups)]
        return shard_low, parts

    def residual(prev, shard_low, ghosts):
        return block_product(local_blocks, columns, prev[0, 0], shard_low, ghosts, ghost_count)[
            None, None
        ]

    grains = dof_count // 3
    factors = jnp.transpose(
        smoother[0, 0].reshape((3, 3, block_count, grains)), (2, 0, 1, 3)
    )
    factors = jnp.broadcast_to(factors[..., None], factors.shape + (vectors,))

    tables = []
    for g in range(groups):
        picked = jnp.take(shaped, send_rows[g], axis=1)
        member = jnp.take(onehot, send_rows[g], axis=1).astype(jnp.bfloat16)
        table = member.T[:, :, None, None] * jnp.transpose(picked, (1, 0, 2))[:, None, :, :]
        tables.append(table.reshape((ghost_count * coarse_rows * dof_count) // vectors, vectors))

    first_iter = point_smooth(smoother, rhs)
    shard_low, parts = outgoing(first_iter)
    first_ghosts = exchange(parts)
    outputs = block_product(
        local_blocks, columns, rhs[0, 0], shard_low, first_ghosts, ghost_count,
        mode="smooth", factors=factors, base=first_iter[0, 0], send=send_rows.reshape(-1),
        tables=tables,
    )
    residual_first, second_iter, shard_low = (o[None, None] for o in outputs[:3])
    shard_low = shard_low[0, 0]
    payloads = list(outputs[3:])
    arrived = exchange(payloads)
    neighbour_tables = [
        a[ghost_rows:].reshape((ghost_count, coarse_rows, dof_count)) for a in arrived
    ]
    residual_second = residual(residual_first, shard_low, arrived)
    local_terms = jnp.einsum(
        "knd,ndr->nkr",
        shaped,
        residual_second[0, 0].astype(jnp.bfloat16),
        preferred_element_type=jnp.float32,
    )
    coarse_residual = jnp.einsum(
        "an,nkr->akr", onehot, local_terms, precision=lax.Precision.HIGHEST
    )
    coarse_rhs = coarse_residual.astype(jnp.bfloat16).reshape((coarse_rows, vectors))
    column_part = gathered_copies(coarse_rhs, "row")
    held = coarse_inverse.reshape((coarse_inverse.shape[0], row_count, col_count, coarse_rows))
    held = lax.dynamic_slice_in_dim(held, lax.axis_index("col"), 1, 2)
    held = held.reshape((coarse_inverse.shape[0], row_count * coarse_rows))
    partial = jnp.dot(held, column_part, preferred_element_type=jnp.float32)
    partial = lax.all_to_all(partial, "col", 0, 0, tiled=True)
    coarse_solution = partial.reshape((col_count, coarse_rows, vectors)).sum(axis=0)
    coarse_flat = coarse_solution.astype(jnp.bfloat16)
    coarse_rounded = coarse_flat.reshape((aggregates, coarse_dofs, vectors))
    neighbour_coarse = exchange([coarse_flat] * groups)
    chosen = jnp.einsum(
        "an,akr->nkr",
        onehot.astype(jnp.bfloat16),
        coarse_rounded,
        preferred_element_type=jnp.float32,
    ).astype(jnp.bfloat16)
    correction = jnp.einsum("knd,nkr->ndr", shaped, chosen, preferred_element_type=jnp.float32)[
        None, None
    ]
    after_coarse = second_iter + correction
    ghost_corrections = [
        jnp.einsum(
            "bjd,jr->bdr", neighbour_tables[g], neighbour_coarse[g],
            preferred_element_type=jnp.float32,
        )
        .astype(jnp.bfloat16)
        .reshape((ghost_rows, vectors))
        for g in range(groups)
    ]
    correction_low = correction.astype(jnp.bfloat16)[0, 0]
    smoothed_solution = block_product(
        local_blocks, columns, residual_second[0, 0], correction_low, ghost_corrections,
        ghost_count, mode="final", factors=factors, base=after_coarse[0, 0],
    )
    return smoothed_solution[None, None]


def solution(mesh):
    placed = (
        P("row", "col", None, None, None),
        P("row", "col", None, None, None),
        P("row", "col", None, None, None),
        P("row", "col", None, None),
        P("row", "col", None, None),
        P("row", "col", None),
        P("row", "col", None, None),
        P("row", None),
    )
    return jax.shard_map(
        cycle,
        mesh=mesh,
        in_specs=placed,
        out_specs=P("row", "col", None, None, None),
        check_vma=False,
    )
```

```python
import functools

import jax
import jax.numpy as jnp
from jax import lax
from jax.experimental import pallas as pl
from jax.experimental.pallas import tpu as pltpu
from jax.sharding import PartitionSpec as P


damping = 0.6


def passed_along(value, axis, steps):
    count = lax.axis_size(axis)
    pairs = [(source, (source + steps) % count) for source in range(count)]
    return lax.ppermute(value, axis, pairs)


def point_smooth(coefficients, vector):
    leading = vector.shape[:2]
    blocks = vector.shape[2]
    grains = vector.shape[3] // 3
    columns = vector.shape[4]
    factors = coefficients.astype(jnp.float32).reshape(leading + (3, 3, blocks, grains))
    pieces = vector.reshape(leading + (blocks, 3, grains, columns))
    outputs = []
    for component in range(3):
        summed = factors[:, :, component, 0, :, :, None] * pieces[:, :, :, 0]
        summed = summed + factors[:, :, component, 1, :, :, None] * pieces[:, :, :, 1]
        summed = summed + factors[:, :, component, 2, :, :, None] * pieces[:, :, :, 2]
        outputs.append(summed)
    return damping * jnp.stack(outputs, axis=3).reshape(vector.shape)


def smoothed(factors_ref, j, vector):
    grains = vector.shape[0] // 3
    pieces = [vector[c * grains:(c + 1) * grains] for c in range(3)]
    outputs = []
    for component in range(3):
        weight = [factors_ref[j, component, c].astype(jnp.float32) for c in range(3)]
        summed = weight[0] * pieces[0]
        summed = summed + weight[1] * pieces[1]
        summed = summed + weight[2] * pieces[2]
        outputs.append(damping * summed)
    return jnp.concatenate(outputs, axis=0)


def product_kernel(
    stored, rows, mode, ghost_total, columns_ref, send_ref, blocks_ref, prev_ref, local_ref, *rest
):
    ghost_refs = rest[:ghost_total]
    rest = rest[ghost_total:]
    if mode == "plain":
        (out_ref, source, picked) = rest
    elif mode == "smooth":
        (factors_ref, base_ref) = rest[:2]
        table_refs = rest[2:2 + ghost_total]
        (out_ref, next_ref, low_ref) = rest[2 + ghost_total:5 + ghost_total]
        payload_refs = rest[5 + ghost_total:5 + 2 * ghost_total]
        (source, picked, kept) = rest[5 + 2 * ghost_total:]
    else:
        (factors_ref, base_ref, out_ref, source, picked) = rest
    n = pl.program_id(0)
    block_count, dof = local_ref.shape[0], local_ref.shape[1]
    ghost_count = (source.shape[0] - block_count) // len(ghost_refs)

    @pl.when(n == 0)
    def _():
        source[0:block_count] = local_ref[...]
        for g, ref in enumerate(ghost_refs):
            for b in range(ghost_count):
                source[block_count + g * ghost_count + b] = ref[b * dof:(b + 1) * dof, :]

    for j in range(rows):
        for k in range(stored):
            picked[k * dof:(k + 1) * dof, :] = source[columns_ref[(n * rows + j) * stored + k]]
        left = prev_ref[j] - jnp.dot(blocks_ref[j], picked[...], preferred_element_type=jnp.float32)
        if mode == "plain":
            out_ref[j] = left
        elif mode == "smooth":
            out_ref[j] = left
            update = smoothed(factors_ref, j, left)
            next_ref[j] = base_ref[j] + update
            low = update.astype(low_ref.dtype)
            low_ref[j] = low
            kept[n * rows + j] = low
        else:
            out_ref[j] = base_ref[j] + smoothed(factors_ref, j, left)

    if mode == "smooth":

        @pl.when(n == pl.num_programs(0) - 1)
        def _():
            for g, ref in enumerate(payload_refs):
                for b in range(ghost_count):
                    ref[b * dof:(b + 1) * dof, :] = kept[send_ref[g * ghost_count + b]]
                ref[ghost_count * dof:, :] = table_refs[g][...]


def block_product(
    blocks, columns, prev, local, ghosts, ghost_count, mode="plain", factors=None, base=None,
    send=None, tables=(),
):
    block_count, dof, width = blocks.shape
    stored = width // dof
    vectors = local.shape[-1]
    rows = 6 if block_count % 6 == 0 else 1
    whole = lambda shape: pl.BlockSpec(shape, lambda n, c, s: (0,) * len(shape))
    tile = pl.BlockSpec((rows, dof, vectors), lambda n, c, s: (n, 0, 0))
    field = jax.ShapeDtypeStruct((block_count, dof, vectors), jnp.float32)
    in_specs = [
        pl.BlockSpec((rows, dof, width), lambda n, c, s: (n, 0, 0)),
        tile,
        whole(local.shape),
    ] + [whole(g.shape) for g in ghosts]
    operands = [blocks, prev, local] + list(ghosts)
    if mode != "plain":
        in_specs += [pl.BlockSpec((rows,) + factors.shape[1:], lambda n, c, s: (n, 0, 0, 0, 0)), tile]
        operands += [factors, base]
    if mode == "smooth":
        in_specs += [whole(t.shape) for t in tables]
        operands += list(tables)
    scratch = [
        pltpu.VMEM((block_count + len(ghosts) * ghost_count, dof, vectors), local.dtype),
        pltpu.VMEM((width, vectors), local.dtype),
    ]
    if send is None:
        send = jnp.zeros((1,), jnp.int32)
    if mode == "smooth":
        payload = [(ghost_count * dof + t.shape[0], vectors) for t in tables]
        out_specs = [tile, tile, tile] + [whole(p) for p in payload]
        out_shape = [
            field,
            field,
            jax.ShapeDtypeStruct(field.shape, jnp.bfloat16),
        ] + [jax.ShapeDtypeStruct(p, jnp.bfloat16) for p in payload]
        scratch.append(pltpu.VMEM((block_count, dof, vectors), jnp.bfloat16))
    else:
        out_specs = tile
        out_shape = field
    grid_spec = pltpu.PrefetchScalarGridSpec(
        num_scalar_prefetch=2,
        grid=(block_count // rows,),
        in_specs=in_specs,
        out_specs=out_specs,
        scratch_shapes=scratch,
    )
    flops = 2 * block_count * dof * width * vectors
    moved = blocks.size * 2 + local.size * 2 * 3 + prev.size * 8 * (1 if mode == "plain" else 3)
    return pl.pallas_call(
        functools.partial(product_kernel, stored, rows, mode, len(ghosts)),
        grid_spec=grid_spec,
        out_shape=out_shape,
        cost_estimate=pl.CostEstimate(flops=flops, bytes_accessed=moved, transcendentals=0),
    )(columns.reshape(-1), send, *operands)


def coarse_kernel(held_ref, part_ref, out_ref):
    out_ref[...] = jnp.dot(held_ref[...], part_ref[...], preferred_element_type=jnp.float32)


def coarse_product(held, part):
    return pl.pallas_call(
        coarse_kernel,
        out_shape=jax.ShapeDtypeStruct((held.shape[0], part.shape[1]), jnp.float32),
    )(held, part)


def gathered_copies(value, axis):
    count = lax.axis_size(axis)
    repeated = jnp.broadcast_to(value[None], (count,) + value.shape)
    repeated = repeated.reshape((count * value.shape[0],) + value.shape[1:])
    return lax.all_to_all(repeated, axis, 0, 0, tiled=True)


def exchange(parts):
    return [
        passed_along(parts[0], "row", 1),
        passed_along(parts[1], "row", -1),
        passed_along(parts[2], "col", 1),
        passed_along(parts[3], "col", -1),
    ]


def cycle(rhs, smoother, blocks, col_index, send_list, agg_id, prolong, coarse_inverse):
    block_count = rhs.shape[2]
    dof_count = rhs.shape[3]
    vectors = rhs.shape[4]
    send_rows = send_list[0, 0]
    groups, ghost_count = send_rows.shape
    coarse_dofs = prolong.shape[2]
    shaped = prolong[0, 0].reshape((coarse_dofs, block_count, dof_count))
    local_blocks = blocks[0, 0]
    columns = col_index[0, 0]
    row_count = lax.axis_size("row")
    col_count = lax.axis_size("col")
    coarse_rows = coarse_inverse.shape[1] // (row_count * col_count)
    aggregates = coarse_rows // coarse_dofs
    onehot = (agg_id[0, 0][None, :] == jnp.arange(aggregates, dtype=jnp.int32)[:, None]).astype(
        jnp.float32
    )

    ghost_rows = ghost_count * dof_count

    def outgoing(vector):
        shard_low = vector.astype(jnp.bfloat16)[0, 0]
        packed = jnp.take(shard_low, send_rows.reshape(-1), axis=0)
        packed = packed.reshape((groups * ghost_rows, vectors))
        parts = [packed[g * ghost_rows:(g + 1) * ghost_rows] for g in range(groups)]
        return shard_low, parts

    def residual(prev, shard_low, ghosts):
        return block_product(local_blocks, columns, prev[0, 0], shard_low, ghosts, ghost_count)[
            None, None
        ]

    grains = dof_count // 3
    factors = jnp.transpose(
        smoother[0, 0].reshape((3, 3, block_count, grains)), (2, 0, 1, 3)
    )
    factors = jnp.broadcast_to(factors[..., None], factors.shape + (vectors,))

    tables = []
    for g in range(groups):
        picked = jnp.take(shaped, send_rows[g], axis=1)
        member = jnp.take(onehot, send_rows[g], axis=1).astype(jnp.bfloat16)
        table = member.T[:, :, None, None] * jnp.transpose(picked, (1, 0, 2))[:, None, :, :]
        tables.append(table.reshape((ghost_count * coarse_rows * dof_count) // vectors, vectors))

    first_iter = point_smooth(smoother, rhs)
    shard_low, parts = outgoing(first_iter)
    first_ghosts = exchange(parts)
    outputs = block_product(
        local_blocks, columns, rhs[0, 0], shard_low, first_ghosts, ghost_count,
        mode="smooth", factors=factors, base=first_iter[0, 0], send=send_rows.reshape(-1),
        tables=tables,
    )
    residual_first, second_iter, shard_low = (o[None, None] for o in outputs[:3])
    shard_low = shard_low[0, 0]
    payloads = list(outputs[3:])
    arrived = exchange(payloads)
    held = coarse_inverse.reshape(
        (coarse_inverse.shape[0], row_count, col_count, coarse_rows)
    )
    held = lax.dynamic_slice_in_dim(held, lax.axis_index("col"), 1, 2)
    held = held.reshape((coarse_inverse.shape[0], row_count * coarse_rows))
    neighbour_tables = [
        a[ghost_rows:].reshape((ghost_count, coarse_rows, dof_count)) for a in arrived
    ]
    residual_second = residual(residual_first, shard_low, arrived)
    local_terms = jnp.einsum(
        "knd,ndr->nkr",
        shaped,
        residual_second[0, 0].astype(jnp.bfloat16),
        preferred_element_type=jnp.float32,
    )
    coarse_residual = jnp.einsum(
        "an,nkr->akr", onehot, local_terms, precision=lax.Precision.HIGHEST
    )
    coarse_rhs = coarse_residual.astype(jnp.bfloat16).reshape((coarse_rows, vectors))
    column_part = gathered_copies(coarse_rhs, "row")
    partial = coarse_product(held, column_part)
    partial = lax.all_to_all(partial, "col", 0, 0, tiled=True)
    coarse_solution = partial.reshape((col_count, coarse_rows, vectors)).sum(axis=0)
    coarse_flat = coarse_solution.astype(jnp.bfloat16)
    coarse_rounded = coarse_flat.reshape((aggregates, coarse_dofs, vectors))
    neighbour_coarse = exchange([coarse_flat] * groups)
    chosen = jnp.einsum(
        "an,akr->nkr",
        onehot.astype(jnp.bfloat16),
        coarse_rounded,
        preferred_element_type=jnp.float32,
    ).astype(jnp.bfloat16)
    correction = jnp.einsum("knd,nkr->ndr", shaped, chosen, preferred_element_type=jnp.float32)[
        None, None
    ]
    after_coarse = second_iter + correction
    ghost_corrections = [
        jnp.einsum(
            "bjd,jr->bdr", neighbour_tables[g], neighbour_coarse[g],
            preferred_element_type=jnp.float32,
        )
        .astype(jnp.bfloat16)
        .reshape((ghost_rows, vectors))
        for g in range(groups)
    ]
    correction_low = correction.astype(jnp.bfloat16)[0, 0]
    smoothed_solution = block_product(
        local_blocks, columns, residual_second[0, 0], correction_low, ghost_corrections,
        ghost_count, mode="final", factors=factors, base=after_coarse[0, 0],
    )
    return smoothed_solution[None, None]


def solution(mesh):
    placed = (
        P("row", "col", None, None, None),
        P("row", "col", None, None, None),
        P("row", "col", None, None, None),
        P("row", "col", None, None),
        P("row", "col", None, None),
        P("row", "col", None),
        P("row", "col", None, None),
        P("row", None),
    )
    return jax.shard_map(
        cycle,
        mesh=mesh,
        in_specs=placed,
        out_specs=P("row", "col", None, None, None),
        check_vma=False,
    )
```

```python
import functools

import jax
import jax.numpy as jnp
from jax import lax
from jax.experimental import pallas as pl
from jax.experimental.pallas import tpu as pltpu
from jax.sharding import PartitionSpec as P


damping = 0.6


def passed_along(value, axis, steps):
    count = lax.axis_size(axis)
    pairs = [(source, (source + steps) % count) for source in range(count)]
    return lax.ppermute(value, axis, pairs)


def point_smooth(coefficients, vector):
    leading = vector.shape[:2]
    blocks = vector.shape[2]
    grains = vector.shape[3] // 3
    columns = vector.shape[4]
    factors = coefficients.astype(jnp.float32).reshape(leading + (3, 3, blocks, grains))
    pieces = vector.reshape(leading + (blocks, 3, grains, columns))
    outputs = []
    for component in range(3):
        summed = factors[:, :, component, 0, :, :, None] * pieces[:, :, :, 0]
        summed = summed + factors[:, :, component, 1, :, :, None] * pieces[:, :, :, 1]
        summed = summed + factors[:, :, component, 2, :, :, None] * pieces[:, :, :, 2]
        outputs.append(summed)
    return damping * jnp.stack(outputs, axis=3).reshape(vector.shape)


def smoothed(factors_ref, j, vector):
    grains = vector.shape[0] // 3
    pieces = [vector[c * grains:(c + 1) * grains] for c in range(3)]
    outputs = []
    for component in range(3):
        weight = [factors_ref[j, component, c].astype(jnp.float32) for c in range(3)]
        summed = weight[0] * pieces[0]
        summed = summed + weight[1] * pieces[1]
        summed = summed + weight[2] * pieces[2]
        outputs.append(damping * summed)
    return jnp.concatenate(outputs, axis=0)


def product_kernel(
    stored, rows, mode, ghost_total, columns_ref, send_ref, blocks_ref, prev_ref, local_ref, *rest
):
    ghost_refs = rest[:ghost_total]
    rest = rest[ghost_total:]
    if mode == "plain":
        (out_ref, source, picked) = rest
    elif mode == "restrict":
        (prolong_ref, out_ref, coarse_ref, source, picked) = rest
    elif mode == "smooth":
        (factors_ref, base_ref) = rest[:2]
        table_refs = rest[2:2 + ghost_total]
        (out_ref, next_ref, low_ref) = rest[2 + ghost_total:5 + ghost_total]
        payload_refs = rest[5 + ghost_total:5 + 2 * ghost_total]
        (source, picked, kept) = rest[5 + 2 * ghost_total:]
    else:
        (factors_ref, base_ref, out_ref, source, picked) = rest
    n = pl.program_id(0)
    block_count, dof = local_ref.shape[0], local_ref.shape[1]
    ghost_count = (source.shape[0] - block_count) // len(ghost_refs)

    @pl.when(n == 0)
    def _():
        if mode == "restrict":
            coarse_ref[...] = jnp.zeros_like(coarse_ref)
        source[0:block_count] = local_ref[...]
        for g, ref in enumerate(ghost_refs):
            for b in range(ghost_count):
                source[block_count + g * ghost_count + b] = ref[b * dof:(b + 1) * dof, :]

    for j in range(rows):
        for k in range(stored):
            picked[k * dof:(k + 1) * dof, :] = source[columns_ref[(n * rows + j) * stored + k]]
        left = prev_ref[j] - jnp.dot(blocks_ref[j], picked[...], preferred_element_type=jnp.float32)
        if mode == "plain":
            out_ref[j] = left
        elif mode == "restrict":
            out_ref[j] = left
            term = jnp.dot(
                prolong_ref[n * rows + j], left.astype(jnp.bfloat16),
                preferred_element_type=jnp.float32,
            )
            owner = send_ref[n * rows + j]
            for a in range(coarse_ref.shape[0]):
                coarse_ref[a] += jnp.where(owner == a, term, 0.0)
        elif mode == "smooth":
            out_ref[j] = left
            update = smoothed(factors_ref, j, left)
            next_ref[j] = base_ref[j] + update
            low = update.astype(low_ref.dtype)
            low_ref[j] = low
            kept[n * rows + j] = low
        else:
            out_ref[j] = base_ref[j] + smoothed(factors_ref, j, left)

    if mode == "smooth":

        @pl.when(n == pl.num_programs(0) - 1)
        def _():
            for g, ref in enumerate(payload_refs):
                for b in range(ghost_count):
                    ref[b * dof:(b + 1) * dof, :] = kept[send_ref[g * ghost_count + b]]
                ref[ghost_count * dof:, :] = table_refs[g][...]


def block_product(
    blocks, columns, prev, local, ghosts, ghost_count, mode="plain", factors=None, base=None,
    send=None, tables=(), prolong=None, aggregates=None,
):
    block_count, dof, width = blocks.shape
    stored = width // dof
    vectors = local.shape[-1]
    rows = 6 if block_count % 6 == 0 else 1
    whole = lambda shape: pl.BlockSpec(shape, lambda n, c, s: (0,) * len(shape))
    tile = pl.BlockSpec((rows, dof, vectors), lambda n, c, s: (n, 0, 0))
    field = jax.ShapeDtypeStruct((block_count, dof, vectors), jnp.float32)
    in_specs = [
        pl.BlockSpec((rows, dof, width), lambda n, c, s: (n, 0, 0)),
        tile,
        whole(local.shape),
    ] + [whole(g.shape) for g in ghosts]
    operands = [blocks, prev, local] + list(ghosts)
    if mode in ("smooth", "final"):
        in_specs += [pl.BlockSpec((rows,) + factors.shape[1:], lambda n, c, s: (n, 0, 0, 0, 0)), tile]
        operands += [factors, base]
    if mode == "smooth":
        in_specs += [whole(t.shape) for t in tables]
        operands += list(tables)
    if mode == "restrict":
        in_specs += [whole(prolong.shape)]
        operands += [prolong]
    scratch = [
        pltpu.VMEM((block_count + len(ghosts) * ghost_count, dof, vectors), local.dtype),
        pltpu.VMEM((width, vectors), local.dtype),
    ]
    if send is None:
        send = jnp.zeros((1,), jnp.int32)
    if mode == "smooth":
        payload = [(ghost_count * dof + t.shape[0], vectors) for t in tables]
        out_specs = [tile, tile, tile] + [whole(p) for p in payload]
        out_shape = [
            field,
            field,
            jax.ShapeDtypeStruct(field.shape, jnp.bfloat16),
        ] + [jax.ShapeDtypeStruct(p, jnp.bfloat16) for p in payload]
        scratch.append(pltpu.VMEM((block_count, dof, vectors), jnp.bfloat16))
    elif mode == "restrict":
        coarse_shape = (aggregates, prolong.shape[1], vectors)
        out_specs = [tile, whole(coarse_shape)]
        out_shape = [field, jax.ShapeDtypeStruct(coarse_shape, jnp.float32)]
    else:
        out_specs = tile
        out_shape = field
    grid_spec = pltpu.PrefetchScalarGridSpec(
        num_scalar_prefetch=2,
        grid=(block_count // rows,),
        in_specs=in_specs,
        out_specs=out_specs,
        scratch_shapes=scratch,
    )
    flops = 2 * block_count * dof * width * vectors
    moved = blocks.size * 2 + local.size * 2 * 3 + prev.size * 8 * (1 if mode == "plain" else 3)
    return pl.pallas_call(
        functools.partial(product_kernel, stored, rows, mode, len(ghosts)),
        grid_spec=grid_spec,
        out_shape=out_shape,
        cost_estimate=pl.CostEstimate(flops=flops, bytes_accessed=moved, transcendentals=0),
    )(columns.reshape(-1), send, *operands)


def coarse_kernel(held_ref, part_ref, out_ref):
    out_ref[...] = jnp.dot(held_ref[...], part_ref[...], preferred_element_type=jnp.float32)


def coarse_product(held, part):
    return pl.pallas_call(
        coarse_kernel,
        out_shape=jax.ShapeDtypeStruct((held.shape[0], part.shape[1]), jnp.float32),
    )(held, part)


def gathered_copies(value, axis):
    count = lax.axis_size(axis)
    repeated = jnp.broadcast_to(value[None], (count,) + value.shape)
    repeated = repeated.reshape((count * value.shape[0],) + value.shape[1:])
    return lax.all_to_all(repeated, axis, 0, 0, tiled=True)


def exchange(parts):
    return [
        passed_along(parts[0], "row", 1),
        passed_along(parts[1], "row", -1),
        passed_along(parts[2], "col", 1),
        passed_along(parts[3], "col", -1),
    ]


def cycle(rhs, smoother, blocks, col_index, send_list, agg_id, prolong, coarse_inverse):
    block_count = rhs.shape[2]
    dof_count = rhs.shape[3]
    vectors = rhs.shape[4]
    send_rows = send_list[0, 0]
    groups, ghost_count = send_rows.shape
    coarse_dofs = prolong.shape[2]
    shaped = prolong[0, 0].reshape((coarse_dofs, block_count, dof_count))
    local_blocks = blocks[0, 0]
    columns = col_index[0, 0]
    row_count = lax.axis_size("row")
    col_count = lax.axis_size("col")
    coarse_rows = coarse_inverse.shape[1] // (row_count * col_count)
    aggregates = coarse_rows // coarse_dofs
    onehot = (agg_id[0, 0][None, :] == jnp.arange(aggregates, dtype=jnp.int32)[:, None]).astype(
        jnp.float32
    )

    ghost_rows = ghost_count * dof_count

    def outgoing(vector):
        shard_low = vector.astype(jnp.bfloat16)[0, 0]
        packed = jnp.take(shard_low, send_rows.reshape(-1), axis=0)
        packed = packed.reshape((groups * ghost_rows, vectors))
        parts = [packed[g * ghost_rows:(g + 1) * ghost_rows] for g in range(groups)]
        return shard_low, parts

    grains = dof_count // 3
    factors = jnp.transpose(
        smoother[0, 0].reshape((3, 3, block_count, grains)), (2, 0, 1, 3)
    )
    factors = jnp.broadcast_to(factors[..., None], factors.shape + (vectors,))

    tables = []
    for g in range(groups):
        picked = jnp.take(shaped, send_rows[g], axis=1)
        member = jnp.take(onehot, send_rows[g], axis=1).astype(jnp.bfloat16)
        table = member.T[:, :, None, None] * jnp.transpose(picked, (1, 0, 2))[:, None, :, :]
        tables.append(table.reshape((ghost_count * coarse_rows * dof_count) // vectors, vectors))

    first_iter = point_smooth(smoother, rhs)
    shard_low, parts = outgoing(first_iter)
    first_ghosts = exchange(parts)
    outputs = block_product(
        local_blocks, columns, rhs[0, 0], shard_low, first_ghosts, ghost_count,
        mode="smooth", factors=factors, base=first_iter[0, 0], send=send_rows.reshape(-1),
        tables=tables,
    )
    residual_first, second_iter, shard_low = (o[None, None] for o in outputs[:3])
    shard_low = shard_low[0, 0]
    payloads = list(outputs[3:])
    arrived = exchange(payloads)
    held = coarse_inverse.reshape(
        (coarse_inverse.shape[0], row_count, col_count, coarse_rows)
    )
    held = lax.dynamic_slice_in_dim(held, lax.axis_index("col"), 1, 2)
    held = held.reshape((coarse_inverse.shape[0], row_count * coarse_rows))
    neighbour_tables = [
        a[ghost_rows:].reshape((ghost_count, coarse_rows, dof_count)) for a in arrived
    ]
    residual_second, coarse_residual = block_product(
        local_blocks, columns, residual_first[0, 0], shard_low, arrived, ghost_count,
        mode="restrict", send=agg_id[0, 0], prolong=jnp.transpose(shaped, (1, 0, 2)),
        aggregates=aggregates,
    )
    residual_second = residual_second[None, None]
    coarse_rhs = coarse_residual.astype(jnp.bfloat16).reshape((coarse_rows, vectors))
    column_part = gathered_copies(coarse_rhs, "row")
    partial = coarse_product(held, column_part)
    partial = lax.all_to_all(partial, "col", 0, 0, tiled=True)
    coarse_solution = partial.reshape((col_count, coarse_rows, vectors)).sum(axis=0)
    coarse_flat = coarse_solution.astype(jnp.bfloat16)
    coarse_rounded = coarse_flat.reshape((aggregates, coarse_dofs, vectors))
    neighbour_coarse = exchange([coarse_flat] * groups)
    chosen = jnp.einsum(
        "an,akr->nkr",
        onehot.astype(jnp.bfloat16),
        coarse_rounded,
        preferred_element_type=jnp.float32,
    ).astype(jnp.bfloat16)
    correction = jnp.einsum("knd,nkr->ndr", shaped, chosen, preferred_element_type=jnp.float32)[
        None, None
    ]
    after_coarse = second_iter + correction
    ghost_corrections = [
        jnp.einsum(
            "bjd,jr->bdr", neighbour_tables[g], neighbour_coarse[g],
            preferred_element_type=jnp.float32,
        )
        .astype(jnp.bfloat16)
        .reshape((ghost_rows, vectors))
        for g in range(groups)
    ]
    correction_low = correction.astype(jnp.bfloat16)[0, 0]
    smoothed_solution = block_product(
        local_blocks, columns, residual_second[0, 0], correction_low, ghost_corrections,
        ghost_count, mode="final", factors=factors, base=after_coarse[0, 0],
    )
    return smoothed_solution[None, None]


def solution(mesh):
    placed = (
        P("row", "col", None, None, None),
        P("row", "col", None, None, None),
        P("row", "col", None, None, None),
        P("row", "col", None, None),
        P("row", "col", None, None),
        P("row", "col", None),
        P("row", "col", None, None),
        P("row", None),
    )
    return jax.shard_map(
        cycle,
        mesh=mesh,
        in_specs=placed,
        out_specs=P("row", "col", None, None, None),
        check_vma=False,
    )
```

```python
import functools

import jax
import jax.numpy as jnp
from jax import lax
from jax.experimental import pallas as pl
from jax.experimental.pallas import tpu as pltpu
from jax.sharding import PartitionSpec as P


damping = 0.6


def passed_along(value, axis, steps):
    count = lax.axis_size(axis)
    pairs = [(source, (source + steps) % count) for source in range(count)]
    return lax.ppermute(value, axis, pairs)


def point_smooth(coefficients, vector):
    leading = vector.shape[:2]
    blocks = vector.shape[2]
    grains = vector.shape[3] // 3
    columns = vector.shape[4]
    factors = coefficients.astype(jnp.float32).reshape(leading + (3, 3, blocks, grains))
    pieces = vector.reshape(leading + (blocks, 3, grains, columns))
    outputs = []
    for component in range(3):
        summed = factors[:, :, component, 0, :, :, None] * pieces[:, :, :, 0]
        summed = summed + factors[:, :, component, 1, :, :, None] * pieces[:, :, :, 1]
        summed = summed + factors[:, :, component, 2, :, :, None] * pieces[:, :, :, 2]
        outputs.append(summed)
    return damping * jnp.stack(outputs, axis=3).reshape(vector.shape)


def smoothed(factors_ref, j, vector):
    grains = vector.shape[0] // 3
    pieces = [vector[c * grains:(c + 1) * grains] for c in range(3)]
    outputs = []
    for component in range(3):
        weight = [factors_ref[j, component, c].astype(jnp.float32) for c in range(3)]
        summed = weight[0] * pieces[0]
        summed = summed + weight[1] * pieces[1]
        summed = summed + weight[2] * pieces[2]
        outputs.append(damping * summed)
    return jnp.concatenate(outputs, axis=0)


def product_kernel(
    stored, rows, mode, ghost_total, columns_ref, send_ref, blocks_ref, prev_ref, local_ref, *rest
):
    ghost_refs = rest[:ghost_total]
    rest = rest[ghost_total:]
    if mode == "plain":
        (out_ref, source, picked) = rest
    elif mode == "smooth":
        (factors_ref, base_ref) = rest[:2]
        table_refs = rest[2:2 + ghost_total]
        (out_ref, next_ref, low_ref) = rest[2 + ghost_total:5 + ghost_total]
        payload_refs = rest[5 + ghost_total:5 + 2 * ghost_total]
        (source, picked, kept) = rest[5 + 2 * ghost_total:]
    else:
        (factors_ref, base_ref, out_ref, source, picked) = rest
    n = pl.program_id(0)
    block_count, dof = local_ref.shape[0], local_ref.shape[1]
    ghost_count = (source.shape[0] - block_count) // len(ghost_refs)

    @pl.when(n == 0)
    def _():
        source[0:block_count] = local_ref[...]
        for g, ref in enumerate(ghost_refs):
            for b in range(ghost_count):
                source[block_count + g * ghost_count + b] = ref[b * dof:(b + 1) * dof, :]

    for j in range(rows):
        for k in range(stored):
            picked[k * dof:(k + 1) * dof, :] = source[columns_ref[(n * rows + j) * stored + k]]
        left = prev_ref[j] - jnp.dot(blocks_ref[j], picked[...], preferred_element_type=jnp.float32)
        if mode == "plain":
            out_ref[j] = left
        elif mode == "smooth":
            out_ref[j] = left
            update = smoothed(factors_ref, j, left)
            next_ref[j] = base_ref[j] + update
            low = update.astype(low_ref.dtype)
            low_ref[j] = low
            kept[n * rows + j] = low
        else:
            out_ref[j] = base_ref[j] + smoothed(factors_ref, j, left)

    if mode == "smooth":

        @pl.when(n == pl.num_programs(0) - 1)
        def _():
            for g, ref in enumerate(payload_refs):
                for b in range(ghost_count):
                    ref[b * dof:(b + 1) * dof, :] = kept[send_ref[g * ghost_count + b]]
                ref[ghost_count * dof:, :] = table_refs[g][...]


def block_product(
    blocks, columns, prev, local, ghosts, ghost_count, mode="plain", factors=None, base=None,
    send=None, tables=(),
):
    block_count, dof, width = blocks.shape
    stored = width // dof
    vectors = local.shape[-1]
    rows = 6 if block_count % 6 == 0 else 1
    whole = lambda shape: pl.BlockSpec(shape, lambda n, c, s: (0,) * len(shape))
    tile = pl.BlockSpec((rows, dof, vectors), lambda n, c, s: (n, 0, 0))
    field = jax.ShapeDtypeStruct((block_count, dof, vectors), jnp.float32)
    in_specs = [
        pl.BlockSpec((rows, dof, width), lambda n, c, s: (n, 0, 0)),
        tile,
        whole(local.shape),
    ] + [whole(g.shape) for g in ghosts]
    operands = [blocks, prev, local] + list(ghosts)
    if mode != "plain":
        in_specs += [pl.BlockSpec((rows,) + factors.shape[1:], lambda n, c, s: (n, 0, 0, 0, 0)), tile]
        operands += [factors, base]
    if mode == "smooth":
        in_specs += [whole(t.shape) for t in tables]
        operands += list(tables)
    scratch = [
        pltpu.VMEM((block_count + len(ghosts) * ghost_count, dof, vectors), local.dtype),
        pltpu.VMEM((width, vectors), local.dtype),
    ]
    if send is None:
        send = jnp.zeros((1,), jnp.int32)
    if mode == "smooth":
        payload = [(ghost_count * dof + t.shape[0], vectors) for t in tables]
        out_specs = [tile, tile, tile] + [whole(p) for p in payload]
        out_shape = [
            field,
            field,
            jax.ShapeDtypeStruct(field.shape, jnp.bfloat16),
        ] + [jax.ShapeDtypeStruct(p, jnp.bfloat16) for p in payload]
        scratch.append(pltpu.VMEM((block_count, dof, vectors), jnp.bfloat16))
    else:
        out_specs = tile
        out_shape = field
    grid_spec = pltpu.PrefetchScalarGridSpec(
        num_scalar_prefetch=2,
        grid=(block_count // rows,),
        in_specs=in_specs,
        out_specs=out_specs,
        scratch_shapes=scratch,
    )
    flops = 2 * block_count * dof * width * vectors
    moved = blocks.size * 2 + local.size * 2 * 3 + prev.size * 8 * (1 if mode == "plain" else 3)
    return pl.pallas_call(
        functools.partial(product_kernel, stored, rows, mode, len(ghosts)),
        grid_spec=grid_spec,
        out_shape=out_shape,
        cost_estimate=pl.CostEstimate(flops=flops, bytes_accessed=moved, transcendentals=0),
    )(columns.reshape(-1), send, *operands)


def coarse_kernel(held_ref, part_ref, out_ref):
    out_ref[...] = jnp.dot(held_ref[...], part_ref[...], preferred_element_type=jnp.float32)


def coarse_product(held, part):
    return pl.pallas_call(
        coarse_kernel,
        out_shape=jax.ShapeDtypeStruct((held.shape[0], part.shape[1]), jnp.float32),
    )(held, part)


def gathered_copies(value, axis):
    count = lax.axis_size(axis)
    repeated = jnp.broadcast_to(value[None], (count,) + value.shape)
    repeated = repeated.reshape((count * value.shape[0],) + value.shape[1:])
    return lax.all_to_all(repeated, axis, 0, 0, tiled=True)


def exchange(parts):
    return [
        passed_along(parts[0], "row", 1),
        passed_along(parts[1], "row", -1),
        passed_along(parts[2], "col", 1),
        passed_along(parts[3], "col", -1),
    ]


def cycle(rhs, smoother, blocks, col_index, send_list, agg_id, prolong, coarse_inverse):
    block_count = rhs.shape[2]
    dof_count = rhs.shape[3]
    vectors = rhs.shape[4]
    send_rows = send_list[0, 0]
    groups, ghost_count = send_rows.shape
    coarse_dofs = prolong.shape[2]
    shaped = prolong[0, 0].reshape((coarse_dofs, block_count, dof_count))
    local_blocks = blocks[0, 0]
    columns = col_index[0, 0]
    row_count = lax.axis_size("row")
    col_count = lax.axis_size("col")
    coarse_rows = coarse_inverse.shape[1] // (row_count * col_count)
    aggregates = coarse_rows // coarse_dofs
    onehot = (agg_id[0, 0][None, :] == jnp.arange(aggregates, dtype=jnp.int32)[:, None]).astype(
        jnp.float32
    )

    ghost_rows = ghost_count * dof_count

    def outgoing(vector):
        shard_low = vector.astype(jnp.bfloat16)[0, 0]
        packed = jnp.take(shard_low, send_rows.reshape(-1), axis=0)
        packed = packed.reshape((groups * ghost_rows, vectors))
        parts = [packed[g * ghost_rows:(g + 1) * ghost_rows] for g in range(groups)]
        return shard_low, parts

    def residual(prev, shard_low, ghosts):
        return block_product(local_blocks, columns, prev[0, 0], shard_low, ghosts, ghost_count)[
            None, None
        ]

    grains = dof_count // 3
    factors = jnp.transpose(
        smoother[0, 0].reshape((3, 3, block_count, grains)), (2, 0, 1, 3)
    )
    factors = jnp.broadcast_to(factors[..., None], factors.shape + (vectors,))

    tables = []
    for g in range(groups):
        picked = jnp.take(shaped, send_rows[g], axis=1)
        member = jnp.take(onehot, send_rows[g], axis=1).astype(jnp.bfloat16)
        table = member.T[:, :, None, None] * jnp.transpose(picked, (1, 0, 2))[:, None, :, :]
        tables.append(table.reshape((ghost_count * coarse_rows * dof_count) // vectors, vectors))

    first_iter = point_smooth(smoother, rhs)
    shard_low, parts = outgoing(first_iter)
    first_ghosts = exchange(parts)
    outputs = block_product(
        local_blocks, columns, rhs[0, 0], shard_low, first_ghosts, ghost_count,
        mode="smooth", factors=factors, base=first_iter[0, 0], send=send_rows.reshape(-1),
        tables=tables,
    )
    residual_first, second_iter, shard_low = (o[None, None] for o in outputs[:3])
    shard_low = shard_low[0, 0]
    payloads = list(outputs[3:])
    arrived = exchange(payloads)
    held = coarse_inverse.reshape(
        (coarse_inverse.shape[0], row_count, col_count, coarse_rows)
    )
    held = lax.dynamic_slice_in_dim(held, lax.axis_index("col"), 1, 2)
    held = held.reshape((coarse_inverse.shape[0], row_count * coarse_rows))
    restrict = onehot.astype(jnp.bfloat16)[:, None, :, None] * shaped[None, :, :, :]
    restrict = restrict.reshape((coarse_rows, block_count * dof_count))
    neighbour_tables = [
        a[ghost_rows:].reshape((ghost_count, coarse_rows, dof_count)) for a in arrived
    ]
    residual_second = residual(residual_first, shard_low, arrived)
    coarse_residual = jnp.dot(
        restrict,
        residual_second[0, 0].astype(jnp.bfloat16).reshape((block_count * dof_count, vectors)),
        preferred_element_type=jnp.float32,
    )
    coarse_rhs = coarse_residual.astype(jnp.bfloat16).reshape((coarse_rows, vectors))
    column_part = gathered_copies(coarse_rhs, "row")
    partial = coarse_product(held, column_part)
    partial = lax.all_to_all(partial, "col", 0, 0, tiled=True)
    coarse_solution = partial.reshape((col_count, coarse_rows, vectors)).sum(axis=0)
    coarse_flat = coarse_solution.astype(jnp.bfloat16)
    coarse_rounded = coarse_flat.reshape((aggregates, coarse_dofs, vectors))
    neighbour_coarse = exchange([coarse_flat] * groups)
    chosen = jnp.einsum(
        "an,akr->nkr",
        onehot.astype(jnp.bfloat16),
        coarse_rounded,
        preferred_element_type=jnp.float32,
    ).astype(jnp.bfloat16)
    correction = jnp.einsum("knd,nkr->ndr", shaped, chosen, preferred_element_type=jnp.float32)[
        None, None
    ]
    after_coarse = second_iter + correction
    ghost_corrections = [
        jnp.einsum(
            "bjd,jr->bdr", neighbour_tables[g], neighbour_coarse[g],
            preferred_element_type=jnp.float32,
        )
        .astype(jnp.bfloat16)
        .reshape((ghost_rows, vectors))
        for g in range(groups)
    ]
    correction_low = correction.astype(jnp.bfloat16)[0, 0]
    smoothed_solution = block_product(
        local_blocks, columns, residual_second[0, 0], correction_low, ghost_corrections,
        ghost_count, mode="final", factors=factors, base=after_coarse[0, 0],
    )
    return smoothed_solution[None, None]


def solution(mesh):
    placed = (
        P("row", "col", None, None, None),
        P("row", "col", None, None, None),
        P("row", "col", None, None, None),
        P("row", "col", None, None),
        P("row", "col", None, None),
        P("row", "col", None),
        P("row", "col", None, None),
        P("row", None),
    )
    return jax.shard_map(
        cycle,
        mesh=mesh,
        in_specs=placed,
        out_specs=P("row", "col", None, None, None),
        check_vma=False,
    )
```
